128 devices in a mesh: req: 32 (over x, y_hi, z), exp: 4 (over y_lo, core).
Axes of the slice: x: 4, y: 4 (y_hi: 2, y_lo: 2; y = y_hi * 2 + y_lo), z: 4, core: 2. Of those that a mesh axis runs over, the one named last changes fastest.
Arguments:
- tokens: bfloat16 [8192, 1024], P('req', 'exp'), may hold values from -7.2 to 7.2
- lengths: int32 [32, 4], P('req'), may hold values from 1 to 128, 256 in all within a row
- groups: int32 [32, 4], P('req'), may hold values from 0 to 3
- owners: int32 [4], replicated, may hold values from 0 to 31, as said below
- prefix_cache: bfloat16 [32, 2048, 2, 1024], P('req', None, None, 'exp'), may hold values from -102 to 102
- attn_gain: float32 [1024], replicated, may hold values from 0.1 to 1.9
- w_qkv: bfloat16 [1024, 3, 1024], P(None, None, 'exp'), may hold values from -0.3125 to 0.3125
- w_out: bfloat16 [1024, 1024], P('exp'), may hold values from -0.1875 to 0.1875
- moe_gain: float32 [1024], replicated, may hold values from 0.1 to 1.9
- w_router: bfloat16 [1024, 16], replicated, may hold values from -0.375 to 0.375
- expert_ids: int32 [8192, 2], P('req'), may hold values from 0 to 15, all different within a row; in each aligned block of 256 rows (0 to 255, 256 to 511, ...) at most 80 rows name the same one
- w_in: bfloat16 [32, 1024, 2, 1408], P('req', None, None, 'exp'), may hold values from -0.1875 to 0.1875
- w_down: bfloat16 [32, 1408, 1024], P('req', 'exp'), may hold values from -0.109375 to 0.109375
Outputs:
- hidden_out: bfloat16 [8192, 1024], P('req', 'exp')
- suffix_kv: bfloat16 [8192, 2, 1024], P('req', None, 'exp')
The draws below stay inside these ranges and needn't reach their ends.
Inputs may be any that keep to these rules, and one draw needn't show every extreme that they name: The 4 lengths of each row sum to 256. `owners`: distinct slots. `expert_ids`: the two experts of a token differ; among the rows of one index of req no expert is named more than 80 times, and some expert exactly that often in some blocks.
All inputs are finite; a program needn't handle non-finite values.
Results may differ from the reference program's by a relative error of at most 0.014.
The reference program's roundings to bfloat16 on the way count: a program that leaves them out, or rounds other values in their place, can miss the bound.
Values may be sent and summed in bfloat16 or wider, within the bound.
No kernel may reach another device: no remote copies, remote signals or barrier semaphores. Data moves between devices by JAX's collectives and lax.ppermute only.
A program may use at most 128 MiB of HBM per device.

```python
import math
import jax
import jax.numpy as jnp
import numpy as np
from jax import lax

D = 1024
HEAD_DIM = 64
FF = 2816
EXPERTS = 16
TOP = 2
SPLIT = 2
GROUPS = 4
PREFIX = 2048
REQ_DEV = 4
TOK_DEV = 256
SUF_MOST = 128
CAP = 40
ROUTE_MOST = 80
HID = 1408
TOKENS = 8192
N_REQ = 32


def draw_tokens(key, part):
    base_key = jax.random.fold_in(key, 29)
    shape = (TOKENS, D)
    place = jnp.arange(D, dtype=jnp.float32) / (D - 1)
    column_scale = 0.6 * jnp.exp(place * jnp.log(3.0))
    values = jnp.clip(jax.random.normal(base_key, shape, jnp.float32), -4.0, 4.0) * column_scale[None, :]
    return values.astype(jnp.bfloat16)


def draw_owners(key, part):
    pick_key, place_key = jax.random.split(jax.random.fold_in(key, 41))
    order = jax.random.permutation(pick_key, jnp.arange(N_REQ - 1, dtype=jnp.int32))[:GROUPS]
    where = jax.random.randint(place_key, (), 0, GROUPS)
    chosen = jnp.where(jnp.arange(GROUPS, dtype=jnp.int32) == where, N_REQ - 1, order)
    return chosen.astype(jnp.int32)


def draw_prefix_cache(key, part):
    base_key = jax.random.fold_in(jax.random.fold_in(key, 17), 0)
    shape = (N_REQ, PREFIX, 2, D)
    values = 1.7 * jnp.clip(jax.random.normal(base_key, shape, jnp.float32), -4.0, 4.0)
    return values.astype(jnp.bfloat16)


def touch_ends(values, rng, smallest, top_value):
    longest = values.shape.index(max(values.shape))
    spots = []
    for shift in (0, 1):
        where = [jax.random.randint(jax.random.fold_in(rng, axis), (), 0, length) for axis, length in enumerate(values.shape)]
        where[longest] = (where[longest] + shift) % values.shape[longest]
        spots.append(tuple(where))
    return values.at[spots[0]].set(smallest).at[spots[1]].set(top_value)


def level_of(rng, dims, shards, least, top_value):
    loudness = 1.0
    for position, parts in shards:
        steps = jax.random.uniform(jax.random.fold_in(jax.random.fold_in(rng, 6), position), (parts,), jnp.float32, least / len(shards), top_value / len(shards))
        loudness = loudness * jnp.repeat(jnp.exp(steps), dims[position] // parts).reshape((-1,) + (1,) * (len(dims) - 1 - position))
    return loudness


def split_up(count, total, bound, skew):
    portions = [(1 << 20) // math.isqrt(grade ** skew) + 1 for grade in range(2, count + 1)]
    surplus, counts = total - bound - (count - 1), [1] * (count - 1)
    while surplus > 0:
        candidates = [i for i in range(count - 1) if counts[i] < bound]
        pool, left = sum([portions[i] for i in candidates]), surplus
        for i in candidates:
            more = min(bound - counts[i], max(1, left * portions[i] // pool), surplus)
            counts[i] = counts[i] + more
            surplus = surplus - more
    return np.array([bound] + counts)


def ragged_sizes(stream_key, amount, total, limit, skew):
    if amount == 2:
        one = jax.random.randint(stream_key, (), max(1, total - limit), min(limit, total - 1) + 1)
        return jnp.stack([one, total - one])
    sizes = jnp.asarray(split_up(amount, total, limit, skew), jnp.int32)
    pairs = (amount - 1) // 2
    giver, taker = sizes[1:1 + 2 * pairs:2], sizes[2:2 + 2 * pairs:2]
    slack = jnp.minimum(giver - 1, limit - taker)
    moved = jax.random.randint(jax.random.fold_in(stream_key, 1), (pairs,), 0, 1 << 20) % (slack + 1)
    sizes = sizes.at[1:1 + 2 * pairs:2].set(giver - moved).at[2:2 + 2 * pairs:2].set(taker + moved)
    return sizes[jax.random.permutation(jax.random.fold_in(stream_key, 2), amount)]


def shared_out(rng, own, number, rows, count, top, limit, slope):
    sequence = jax.random.permutation(rng, count)
    heavy_load, common = portions_of(count, rows * top, limit, slope, True), portions_of(count, rows * top, limit, slope, False)
    places = jnp.arange(count)

    def named(sizes, offset_by):
        used = int((sizes > 0).sum())
        fixed = max(1, used // 4)
        passed = fixed + (places - fixed + offset_by * (used - fixed)) % max(1, count - fixed)
        return jnp.zeros((count,), jnp.int32).at[sequence[jnp.where(places < fixed, places, passed)]].set(jnp.asarray(sizes, jnp.int32))

    sizes = jnp.where(number % 4 == 0, named(heavy_load, number // 4), named(common, number - number // 4 - 1))
    mixed = jax.random.permutation(jax.random.fold_in(own, 3), count)
    giver, sink = mixed[0:count // 2 * 2:2], mixed[1:count // 2 * 2:2]
    room = jnp.minimum(sizes[giver] - 1, limit - sizes[sink]) // 2
    room = jnp.where((giver == sequence[0]) | (sink == sequence[0]) | (sizes[sink] == 0), 0, jnp.maximum(room, 0))
    passed = jax.random.randint(jax.random.fold_in(own, 4), (count // 2,), 0, 1 << 20) % (room + 1)
    sizes = sizes.at[giver].add(-passed).at[sink].add(passed)
    members = jnp.searchsorted(jnp.cumsum(sizes), jnp.arange(rows * top), side="right").astype(jnp.int32)
    listing = members.reshape(top, rows).T
    listing = listing[jax.random.permutation(jax.random.fold_in(own, 1), rows)]
    offset_by = jax.random.randint(jax.random.fold_in(own, 2), (rows, 1), 0, top)
    return jnp.take_along_axis(listing, (jnp.arange(top)[None, :] + offset_by) % top, axis=1)


def portions_of(number_of, total, bound, skew, full):
    weights = [(1 << 20) // math.isqrt(grade ** skew) + 1 for grade in range(1, number_of + 1)]
    largest = bound if full else min(bound, max(-(-total // number_of), total * weights[0] // sum(weights)))
    least = 1 if total - largest >= number_of - 1 else 0
    holding, spare = [largest] + [least] * (number_of - 1), total - largest - least * (number_of - 1)
    while spare > 0:
        free = [i for i in range(1, number_of) if holding[i] < largest] or [i for i in range(1, number_of) if holding[i] < bound]
        whole, budget = sum([weights[i] for i in free]), spare
        for i in free:
            more = min(bound - holding[i], max(1, budget * weights[i] // whole), spare)
            holding[i] = holding[i] + more
            spare = spare - more
    return np.array(holding)


def centred(stream_key, dims, width, limit, shards=(), kind=jnp.bfloat16):
    values = width * jax.random.normal(stream_key, dims, jnp.float32)
    if shards:
        values = values * level_of(stream_key, dims, shards, -0.22, 0.18)
    return jnp.clip(values, -limit, limit).astype(kind)


def setup_inputs(seed: int = 0) -> dict:
    key_of = jax.random.split(jax.random.key(seed), 14)
    tokens = draw_tokens(jax.random.fold_in(key_of[13], 71), 0)
    lengths = jax.vmap(lambda own: ragged_sizes(own, REQ_DEV, TOK_DEV, SUF_MOST, 2))(jax.random.split(key_of[1], N_REQ)).reshape((N_REQ, REQ_DEV)).astype(jnp.int32)
    groups = touch_ends(jax.random.randint(key_of[2], (N_REQ, REQ_DEV), 0, GROUPS), jax.random.fold_in(key_of[2], 1), 0, GROUPS - 1).astype(jnp.int32)
    owners = draw_owners(jax.random.fold_in(key_of[13], 71), 0)
    prefix_cache = draw_prefix_cache(jax.random.fold_in(key_of[13], 71), 0)
    attn_gain = jnp.clip(1.0 + 0.18 * jax.random.normal(key_of[5], (D,), jnp.float32), 0.1, 1.9)
    w_qkv = centred(key_of[6], (D, 3, D), (D // 3) ** -0.5, 0.3125, ((2, 4),))
    w_out = centred(key_of[7], (D, D), D ** -0.5, 0.1875, ((0, 4),))
    moe_gain = jnp.clip(1.0 + 0.18 * jax.random.normal(key_of[8], (D,), jnp.float32), 0.1, 1.9)
    w_router = centred(key_of[9], (D, EXPERTS), (D // 4) ** -0.5, 0.375)
    expert_ids_keys = jax.random.split(jax.random.fold_in(key_of[10], 1), TOKENS // TOK_DEV)
    expert_ids_turns = jax.random.permutation(jax.random.fold_in(key_of[10], 3), TOKENS // TOK_DEV)
    expert_ids = jax.vmap(lambda own, number: shared_out(jax.random.fold_in(key_of[10], 2), own, number, TOK_DEV, EXPERTS, TOP, ROUTE_MOST, 2))(expert_ids_keys, expert_ids_turns).reshape((TOKENS, TOP))
    w_in = centred(key_of[11], (EXPERTS * SPLIT, D, 2, HID), D ** -0.5, 0.1875, ((0, 32), (3, 4)))
    w_down = centred(key_of[12], (EXPERTS * SPLIT, HID, D), FF ** -0.5, 0.109375, ((0, 32), (1, 4)))
    return {"tokens": tokens, "lengths": lengths, "groups": groups, "owners": owners, "prefix_cache": prefix_cache, "attn_gain": attn_gain, "w_qkv": w_qkv, "w_out": w_out, "moe_gain": moe_gain, "w_router": w_router, "expert_ids": expert_ids, "w_in": w_in, "w_down": w_down}


epsilon = 1e-06

def norm_rows(values, gain):
    squares = lax.optimization_barrier(jnp.sum(values * values, axis=1))
    return values * lax.rsqrt(squares / values.shape[1] + epsilon)[:, None] * gain

def request_context(query_all, key_all, value_all, prefix_kv, start, length, window):
    row_count = query_all.shape[0]
    first = jnp.minimum(start, row_count - window).astype(jnp.int32)
    query_win = lax.dynamic_slice_in_dim(query_all, first, window, 0).astype(jnp.float32)
    key_win = lax.dynamic_slice_in_dim(key_all, first, window, 0).astype(jnp.float32)
    value_win = lax.dynamic_slice_in_dim(value_all, first, window, 0).astype(jnp.float32)
    keys = jnp.concatenate([prefix_kv[:, 0].astype(jnp.float32), key_win], axis=0)
    values = jnp.concatenate([prefix_kv[:, 1].astype(jnp.float32), value_win], axis=0)
    scores = jnp.einsum('qhd,khd->hqk', query_win, keys) / math.sqrt(query_all.shape[2])
    positions = first + jnp.arange(window, dtype=jnp.int32)
    suffix_ok = (positions[None, :] <= positions[:, None]) & (positions[None, :] >= start)
    allowed = jnp.concatenate([jnp.ones((window, prefix_kv.shape[0]), bool), suffix_ok], axis=1)
    scores = jnp.where(allowed[None], scores, -1e+30)
    highest = lax.optimization_barrier(jnp.max(scores, axis=-1, keepdims=True))
    weight = jnp.exp(scores - highest)
    totals = lax.optimization_barrier(jnp.sum(weight, axis=-1))
    rounded = lax.optimization_barrier(weight.astype(jnp.bfloat16)).astype(jnp.float32)
    context = jnp.einsum('hqk,khd->qhd', rounded, values) / jnp.transpose(totals)[:, :, None]
    inside = (positions >= start) & (positions < start + length)
    context = context * inside[:, None, None].astype(jnp.float32)
    placed = jnp.zeros((row_count,) + context.shape[1:], jnp.float32)
    return lax.dynamic_update_slice_in_dim(placed, context, first, 0)

def slot_ranks(identity, experts):
    flat_ids = identity.reshape(-1).astype(jnp.int32)
    hits = (flat_ids[:, None] == jnp.arange(experts, dtype=jnp.int32)[None, :]).astype(jnp.int32)
    before = jnp.cumsum(hits, axis=0) - hits
    return (flat_ids, lax.optimization_barrier(jnp.sum(before * hits, axis=1)).astype(jnp.int32))

def slot_table(flat_ids, ranks, capacity, experts, row_count, topk):
    kept = ranks < capacity
    target = jnp.where(kept, flat_ids * capacity + ranks, experts * capacity).astype(jnp.int32)
    source = (jnp.arange(flat_ids.shape[0], dtype=jnp.int32) // topk).astype(jnp.int32)
    table = jnp.full((experts * capacity,), row_count, jnp.int32).at[target].set(source, mode='drop')
    return (kept, table)

def reference(tokens, lengths, groups, owners, prefix_cache, attn_gain, w_qkv, w_out, moe_gain, w_router, expert_ids, w_in, w_down):
    blocks = tokens.reshape(N_REQ, TOK_DEV, D)
    local_heads = D // HEAD_DIM

    def section(packed):
        block_tokens, block_lengths, block_groups = packed
        x_attn = norm_rows(block_tokens.astype(jnp.float32), attn_gain).astype(jnp.bfloat16)
        qkv = jnp.dot(x_attn, w_qkv.reshape(D, 3 * D), preferred_element_type=jnp.float32)
        qkv = qkv.astype(jnp.bfloat16).reshape(TOK_DEV, 3, D)
        query_all = qkv[:, 0].reshape(TOK_DEV, local_heads, HEAD_DIM)
        key_all = qkv[:, 1].reshape(TOK_DEV, local_heads, HEAD_DIM)
        value_all = qkv[:, 2].reshape(TOK_DEV, local_heads, HEAD_DIM)
        starts = (jnp.cumsum(block_lengths) - block_lengths).astype(jnp.int32)
        context = jnp.zeros((TOK_DEV, local_heads, HEAD_DIM), jnp.float32)
        for request in range(REQ_DEV):
            slot = owners[block_groups[request]]
            prefix_kv = prefix_cache[slot].reshape(PREFIX, 2, local_heads, HEAD_DIM)
            context = context + request_context(query_all, key_all, value_all, prefix_kv, starts[request], block_lengths[request], SUF_MOST)
        context = context.reshape(TOK_DEV, D).astype(jnp.bfloat16)
        resid = block_tokens.astype(jnp.float32) + jnp.dot(context, w_out, preferred_element_type=jnp.float32)
        x_moe = norm_rows(resid, moe_gain).astype(jnp.bfloat16)
        suffix = jnp.stack([qkv[:, 1], qkv[:, 2]], axis=1)
        return (resid, x_moe, suffix)
    resid, x_moe, suffix = lax.map(section, (blocks, lengths, groups))
    block_ids = expert_ids.reshape(N_REQ, TOK_DEV, TOP)

    def route(packed):
        block_x, block_id = packed
        logits = jnp.dot(block_x, w_router, preferred_element_type=jnp.float32)
        gates = jax.nn.sigmoid(jnp.take_along_axis(logits, block_id, axis=1)).reshape(-1)
        flat_ids, ranks = slot_ranks(block_id, EXPERTS)
        kept, table = slot_table(flat_ids, ranks, CAP, EXPERTS, TOK_DEV, TOP)
        padded = jnp.concatenate([block_x, jnp.zeros((1, D), block_x.dtype)], axis=0)
        return (gates, flat_ids, ranks, kept, padded[table].reshape(EXPERTS, CAP, D))
    gates, flat_ids, ranks, kept, sent = lax.map(route, (x_moe, block_ids))
    per_expert = jnp.transpose(sent, (1, 0, 2, 3)).reshape(EXPERTS, N_REQ * CAP, D)
    w_in_expert = w_in.reshape(EXPERTS, SPLIT, D, 2, FF // SPLIT)
    w_down_expert = w_down.reshape(EXPERTS, FF, D)

    def expert(packed):
        expert_rows, weight_in, weight_down = packed
        joined = jnp.transpose(weight_in, (1, 2, 0, 3))
        gate_part = jnp.dot(expert_rows, joined[:, 0].reshape(D, FF), preferred_element_type=jnp.float32)
        up_part = jnp.dot(expert_rows, joined[:, 1].reshape(D, FF), preferred_element_type=jnp.float32)
        units = (jax.nn.gelu(gate_part, approximate=True) * up_part).astype(jnp.bfloat16)
        return jnp.dot(units, weight_down, preferred_element_type=jnp.float32)
    results = lax.map(expert, (per_expert, w_in_expert, w_down_expert))
    results = jnp.transpose(results.reshape(EXPERTS, N_REQ, CAP, D), (1, 0, 2, 3)).reshape(N_REQ, EXPERTS * CAP, D)

    def finish(packed):
        block_out, block_gates, block_flat, block_ranks, block_kept, block_resid = packed
        source = (block_flat * CAP + jnp.minimum(block_ranks, CAP - 1)).astype(jnp.int32)
        picked = block_out[source].reshape(TOK_DEV, TOP, D)
        scale = jnp.where(block_kept, block_gates, 0.0).reshape(TOK_DEV, TOP)
        return (block_resid + lax.optimization_barrier(jnp.sum(picked * scale[:, :, None], axis=1))).astype(jnp.bfloat16)
    hidden = lax.map(finish, (results, gates, flat_ids, ranks, kept, resid))
    return (hidden.reshape(TOKENS, D), suffix.reshape(TOKENS, 2, D))
```

```python
import math

import jax
import jax.numpy as jnp
from jax import lax
from jax.sharding import PartitionSpec as P

HEAD_DIM = 64
EXPERTS = 16
TOP = 2
SPLIT = 2
GROUPS = 4
PREFIX = 2048
REQ_DEV = 4
SUF_MOST = 128
CAP = 40


epsilon = 1e-06


def spread(shard, axis, root):
    mine = lax.axis_index(axis) == root
    return lax.psum(jnp.where(mine, shard, jnp.zeros_like(shard)), axis)


def norm_rows(values, gain):
    squares = jnp.sum(values * values, axis=1)
    return values * lax.rsqrt(squares / values.shape[1] + epsilon)[:, None] * gain


def request_context(query_all, key_all, value_all, prefix_kv, start, length, window):
    row_count = query_all.shape[0]
    first = jnp.minimum(start, row_count - window)
    query_win = lax.dynamic_slice_in_dim(query_all, first, window, 0)
    key_win = lax.dynamic_slice_in_dim(key_all, first, window, 0)
    value_win = lax.dynamic_slice_in_dim(value_all, first, window, 0)
    keys = jnp.concatenate([prefix_kv[:, 0], key_win], axis=0)
    values = jnp.concatenate([prefix_kv[:, 1], value_win], axis=0)
    scores = jnp.einsum(
        "qhd,khd->hqk", query_win, keys, preferred_element_type=jnp.float32
    ) / math.sqrt(query_all.shape[2])
    positions = first + jnp.arange(window, dtype=jnp.int32)
    suffix_ok = (positions[None, :] <= positions[:, None]) & (positions[None, :] >= start)
    allowed = jnp.concatenate([jnp.ones((window, prefix_kv.shape[0]), bool), suffix_ok], axis=1)
    scores = jnp.where(allowed[None], scores, -1e30)
    highest = jnp.max(scores, axis=-1, keepdims=True)
    weight = jnp.exp(scores - highest)
    totals = jnp.sum(weight, axis=-1)
    context = jnp.einsum(
        "hqk,khd->qhd", weight.astype(jnp.bfloat16), values, preferred_element_type=jnp.float32
    )
    context = context / jnp.transpose(totals)[:, :, None]
    inside = (positions >= start) & (positions < start + length)
    context = context * inside[:, None, None].astype(jnp.float32)
    placed = jnp.zeros((row_count,) + context.shape[1:], jnp.float32)
    return lax.dynamic_update_slice_in_dim(placed, context, first, 0)


def slot_ranks(identity, experts):
    flat_ids = identity.reshape(-1)
    hits = (flat_ids[:, None] == jnp.arange(experts, dtype=jnp.int32)[None, :]).astype(jnp.int32)
    before = jnp.cumsum(hits, axis=0) - hits
    return (flat_ids, jnp.sum(before * hits, axis=1))


def slot_table(flat_ids, ranks, capacity, experts, row_count, topk):
    kept = ranks < capacity
    target = jnp.where(kept, flat_ids * capacity + ranks, experts * capacity)
    source = jnp.arange(flat_ids.shape[0], dtype=jnp.int32) // topk
    table = (
        jnp.full((experts * capacity,), row_count, jnp.int32).at[target].set(source, mode="drop")
    )
    return (kept, table)


def expert_apply(slots, weight_in, weight_down):
    joined = jnp.einsum("slcd,ldgh->slcgh", slots, weight_in, preferred_element_type=jnp.float32)
    units = (jax.nn.gelu(joined[:, :, :, 0], approximate=True) * joined[:, :, :, 1]).astype(
        jnp.bfloat16
    )
    return jnp.einsum("slch,lhd->slcd", units, weight_down, preferred_element_type=jnp.float32)


def shards(
    tokens,
    lengths,
    groups,
    owners,
    prefix_cache,
    attn_gain,
    w_qkv,
    w_out,
    moe_gain,
    w_router,
    expert_ids,
    w_in,
    w_down,
):
    rows_whole = lax.all_gather(tokens, "exp", axis=1, tiled=True)
    row_count = rows_whole.shape[0]
    full_width = rows_whole.shape[1]
    quarter = tokens.shape[1]
    local_heads = quarter // HEAD_DIM
    x_attn = norm_rows(rows_whole.astype(jnp.float32), attn_gain).astype(jnp.bfloat16)
    qkv = jnp.dot(
        x_attn, w_qkv.reshape(full_width, 3 * quarter), preferred_element_type=jnp.float32
    )
    qkv = qkv.astype(jnp.bfloat16).reshape(row_count, 3, quarter)
    suffix_kv = jnp.stack([qkv[:, 1], qkv[:, 2]], axis=1)
    query_all = qkv[:, 0].reshape(row_count, local_heads, HEAD_DIM)
    key_all = qkv[:, 1].reshape(row_count, local_heads, HEAD_DIM)
    value_all = qkv[:, 2].reshape(row_count, local_heads, HEAD_DIM)
    own_slot = prefix_cache[0]
    block_lengths = lengths[0]
    block_groups = groups[0]
    starts = jnp.cumsum(block_lengths) - block_lengths
    context = jnp.zeros((row_count, local_heads, HEAD_DIM), jnp.float32)
    req_total = lax.axis_size("req")
    pieces = own_slot.reshape(req_total, PREFIX // req_total, 2, quarter)
    pieces = lax.all_to_all(pieces, "req", split_axis=0, concat_axis=0, tiled=True)
    owned = jnp.take(pieces, owners, axis=0)
    cached = lax.all_gather(owned, "req", axis=1, tiled=True)
    for request in range(REQ_DEV):
        prefix_kv = cached[block_groups[request]].reshape(PREFIX, 2, local_heads, HEAD_DIM)
        context = context + request_context(
            query_all,
            key_all,
            value_all,
            prefix_kv,
            starts[request],
            block_lengths[request],
            SUF_MOST,
        )
    context = context.reshape(row_count, quarter).astype(jnp.bfloat16)
    partial_attn = jnp.dot(context, w_out, preferred_element_type=jnp.float32)
    resid = tokens.astype(jnp.float32) + lax.psum_scatter(
        partial_attn.astype(jnp.bfloat16), "exp", scatter_dimension=1, tiled=True
    ).astype(jnp.float32)
    squares = lax.psum(jnp.sum(resid * resid, axis=1), "exp")
    column_start = lax.axis_index("exp") * quarter
    gain_part = lax.dynamic_slice_in_dim(moe_gain, column_start, quarter, 0)
    x_part = (resid * lax.rsqrt(squares / full_width + epsilon)[:, None] * gain_part).astype(
        jnp.bfloat16
    )
    x_source = lax.all_gather(x_part, "exp", axis=1, tiled=True)
    logits = jnp.dot(x_source, w_router, preferred_element_type=jnp.float32)
    gates = jax.nn.sigmoid(jnp.take_along_axis(logits, expert_ids, axis=1)).reshape(-1)
    flat_ids, ranks = slot_ranks(expert_ids, EXPERTS)
    kept, table = slot_table(flat_ids, ranks, CAP, EXPERTS, row_count, TOP)
    columns = x_source.shape[1]
    padded = jnp.concatenate([x_source, jnp.zeros((1, columns), x_source.dtype)], axis=0)
    picked = padded[table].reshape(EXPERTS, 1, CAP, columns)
    local_rows = EXPERTS * SPLIT // req_total
    outgoing_rows = jnp.broadcast_to(picked, (EXPERTS, SPLIT, CAP, columns)).reshape(
        req_total, local_rows, CAP, columns
    )
    partial_out = expert_apply(
        lax.all_to_all(outgoing_rows, "req", split_axis=0, concat_axis=0, tiled=True), w_in, w_down
    )
    returned = lax.all_to_all(
        partial_out.astype(jnp.bfloat16), "req", split_axis=0, concat_axis=0, tiled=True
    ).astype(partial_out.dtype)
    out_columns = returned.shape[3]
    summed = jnp.sum(returned.reshape(EXPERTS, SPLIT, CAP, out_columns), axis=1).reshape(
        EXPERTS * CAP, out_columns
    )
    source = flat_ids * CAP + jnp.minimum(ranks, CAP - 1)
    chosen = summed[source].reshape(row_count, TOP, out_columns)
    scale = jnp.where(kept, gates, 0.0).reshape(row_count, TOP)
    mixture = jnp.sum(chosen * scale[:, :, None], axis=1)
    moe_part = lax.psum_scatter(
        mixture.astype(jnp.bfloat16), "exp", scatter_dimension=1, tiled=True
    ).astype(jnp.float32)
    hidden_out = (resid + moe_part).astype(jnp.bfloat16)
    return (hidden_out, suffix_kv)


def solution(mesh):
    return jax.shard_map(
        shards,
        mesh=mesh,
        in_specs=(
            P("req", "exp"),
            P("req", None),
            P("req", None),
            P(),
            P("req", None, None, "exp"),
            P(),
            P(None, None, "exp"),
            P("exp", None),
            P(),
            P(),
            P("req", None),
            P("req", None, None, "exp"),
            P("req", "exp", None),
        ),
        out_specs=(P("req", "exp"), P("req", None, "exp")),
        check_vma=False,
    )
```

```python
import math

import jax
import jax.numpy as jnp
from jax import lax
from jax.sharding import PartitionSpec as P

HEAD_DIM = 64
EXPERTS = 16
TOP = 2
SPLIT = 2
GROUPS = 4
PREFIX = 2048
REQ_DEV = 4
SUF_MOST = 128
CAP = 40


epsilon = 1e-06


def spread(shard, axis, root):
    mine = lax.axis_index(axis) == root
    return lax.psum(jnp.where(mine, shard, jnp.zeros_like(shard)), axis)


def norm_rows(values, gain):
    squares = jnp.sum(values * values, axis=1)
    return values * lax.rsqrt(squares / values.shape[1] + epsilon)[:, None] * gain


def request_context(query_all, key_all, value_all, prefix_kv, start, length, window):
    row_count = query_all.shape[0]
    first = jnp.minimum(start, row_count - window)
    query_win = lax.dynamic_slice_in_dim(query_all, first, window, 0)
    key_win = lax.dynamic_slice_in_dim(key_all, first, window, 0)
    value_win = lax.dynamic_slice_in_dim(value_all, first, window, 0)
    keys = jnp.concatenate([prefix_kv[:, 0], key_win], axis=0)
    values = jnp.concatenate([prefix_kv[:, 1], value_win], axis=0)
    scores = jnp.einsum(
        "qhd,khd->hqk", query_win, keys, preferred_element_type=jnp.float32
    ) / math.sqrt(query_all.shape[2])
    positions = first + jnp.arange(window, dtype=jnp.int32)
    suffix_ok = (positions[None, :] <= positions[:, None]) & (positions[None, :] >= start)
    allowed = jnp.concatenate([jnp.ones((window, prefix_kv.shape[0]), bool), suffix_ok], axis=1)
    scores = jnp.where(allowed[None], scores, -1e30)
    highest = jnp.max(scores, axis=-1, keepdims=True)
    weight = jnp.exp(scores - highest)
    totals = jnp.sum(weight, axis=-1)
    context = jnp.einsum(
        "hqk,khd->qhd", weight.astype(jnp.bfloat16), values, preferred_element_type=jnp.float32
    )
    context = context / jnp.transpose(totals)[:, :, None]
    inside = (positions >= start) & (positions < start + length)
    context = context * inside[:, None, None].astype(jnp.float32)
    placed = jnp.zeros((row_count,) + context.shape[1:], jnp.float32)
    return lax.dynamic_update_slice_in_dim(placed, context, first, 0)


def slot_ranks(identity, experts):
    flat_ids = identity.reshape(-1)
    hits = (flat_ids[:, None] == jnp.arange(experts, dtype=jnp.int32)[None, :]).astype(jnp.int32)
    before = jnp.cumsum(hits, axis=0) - hits
    return (flat_ids, jnp.sum(before * hits, axis=1))


def slot_table(flat_ids, ranks, capacity, experts, row_count, topk):
    kept = ranks < capacity
    target = jnp.where(kept, flat_ids * capacity + ranks, experts * capacity)
    source = jnp.arange(flat_ids.shape[0], dtype=jnp.int32) // topk
    table = (
        jnp.full((experts * capacity,), row_count, jnp.int32).at[target].set(source, mode="drop")
    )
    return (kept, table)


def expert_apply(slots, weight_in, weight_down):
    joined = jnp.einsum("slcd,ldgh->slcgh", slots, weight_in, preferred_element_type=jnp.float32)
    units = (jax.nn.gelu(joined[:, :, :, 0], approximate=True) * joined[:, :, :, 1]).astype(
        jnp.bfloat16
    )
    return jnp.einsum("slch,lhd->slcd", units, weight_down, preferred_element_type=jnp.float32)


def shards(
    tokens,
    lengths,
    groups,
    owners,
    prefix_cache,
    attn_gain,
    w_qkv,
    w_out,
    moe_gain,
    w_router,
    expert_ids,
    w_in,
    w_down,
):
    rows_whole = lax.all_gather(tokens, "exp", axis=1, tiled=True)
    row_count = rows_whole.shape[0]
    full_width = rows_whole.shape[1]
    quarter = tokens.shape[1]
    local_heads = quarter // HEAD_DIM
    x_attn = norm_rows(rows_whole.astype(jnp.float32), attn_gain).astype(jnp.bfloat16)
    qkv = jnp.dot(
        x_attn, w_qkv.reshape(full_width, 3 * quarter), preferred_element_type=jnp.float32
    )
    qkv = qkv.astype(jnp.bfloat16).reshape(row_count, 3, quarter)
    suffix_kv = jnp.stack([qkv[:, 1], qkv[:, 2]], axis=1)
    query_all = qkv[:, 0].reshape(row_count, local_heads, HEAD_DIM)
    key_all = qkv[:, 1].reshape(row_count, local_heads, HEAD_DIM)
    value_all = qkv[:, 2].reshape(row_count, local_heads, HEAD_DIM)
    own_slot = prefix_cache[0]
    block_lengths = lengths[0]
    block_groups = groups[0]
    starts = jnp.cumsum(block_lengths) - block_lengths
    context = jnp.zeros((row_count, local_heads, HEAD_DIM), jnp.float32)
    req_total = lax.axis_size("req")
    pieces = own_slot.reshape(req_total, PREFIX // req_total, 2, quarter)
    pieces = lax.all_to_all(pieces, "req", split_axis=0, concat_axis=0, tiled=True)
    owned = jnp.take(pieces, owners, axis=0)
    cached = lax.all_gather(owned, "req", axis=1, tiled=True)
    for request in range(REQ_DEV):
        prefix_kv = cached[block_groups[request]].reshape(PREFIX, 2, local_heads, HEAD_DIM)
        context = context + request_context(
            query_all,
            key_all,
            value_all,
            prefix_kv,
            starts[request],
            block_lengths[request],
            SUF_MOST,
        )
    context = context.reshape(row_count, quarter).astype(jnp.bfloat16)
    partial_attn = jnp.dot(context, w_out, preferred_element_type=jnp.float32)
    attn_full = lax.psum(partial_attn.astype(jnp.bfloat16), "exp").astype(jnp.float32)
    resid_full = rows_whole.astype(jnp.float32) + attn_full
    x_full = norm_rows(resid_full, moe_gain).astype(jnp.bfloat16)
    column_start = lax.axis_index("exp") * quarter
    resid = lax.dynamic_slice_in_dim(resid_full, column_start, quarter, 1)
    x_part = lax.dynamic_slice_in_dim(x_full, column_start, quarter, 1)
    logits = jnp.dot(x_full, w_router, preferred_element_type=jnp.float32)
    gates = jax.nn.sigmoid(jnp.take_along_axis(logits, expert_ids, axis=1)).reshape(-1)
    flat_ids, ranks = slot_ranks(expert_ids, EXPERTS)
    kept, table = slot_table(flat_ids, ranks, CAP, EXPERTS, row_count, TOP)
    padded = jnp.concatenate([x_part, jnp.zeros((1, quarter), x_part.dtype)], axis=0)
    picked = padded[table].reshape(EXPERTS, 1, CAP, quarter)
    local_rows = EXPERTS * SPLIT // req_total
    outgoing_rows = jnp.broadcast_to(picked, (EXPERTS, SPLIT, CAP, quarter)).reshape(
        req_total, local_rows, CAP, quarter
    )
    arrived = lax.all_to_all(outgoing_rows, "req", split_axis=0, concat_axis=0, tiled=True)
    arrived = lax.all_gather(arrived, "exp", axis=3, tiled=True)
    partial_out = expert_apply(arrived, w_in, w_down)
    reduced = lax.psum_scatter(
        partial_out.astype(jnp.bfloat16), "exp", scatter_dimension=3, tiled=True
    )
    returned = lax.all_to_all(reduced, "req", split_axis=0, concat_axis=0, tiled=True).astype(
        jnp.float32
    )
    summed = jnp.sum(returned.reshape(EXPERTS, SPLIT, CAP, quarter), axis=1).reshape(
        EXPERTS * CAP, quarter
    )
    source = flat_ids * CAP + jnp.minimum(ranks, CAP - 1)
    chosen = summed[source].reshape(row_count, TOP, quarter)
    scale = jnp.where(kept, gates, 0.0).reshape(row_count, TOP)
    mixture = jnp.sum(chosen * scale[:, :, None], axis=1)
    hidden_out = (resid + mixture).astype(jnp.bfloat16)
    return (hidden_out, suffix_kv)


def solution(mesh):
    return jax.shard_map(
        shards,
        mesh=mesh,
        in_specs=(
            P("req", "exp"),
            P("req", None),
            P("req", None),
            P(),
            P("req", None, None, "exp"),
            P(),
            P(None, None, "exp"),
            P("exp", None),
            P(),
            P(),
            P("req", None),
            P("req", None, None, "exp"),
            P("req", "exp", None),
        ),
        out_specs=(P("req", "exp"), P("req", None, "exp")),
        check_vma=False,
    )
```

```python
import math

import jax
import jax.numpy as jnp
from jax import lax
from jax.sharding import PartitionSpec as P
from jax.experimental import pallas as pl
from jax.experimental.pallas import tpu as pltpu

HEAD_DIM = 64
EXPERTS = 16
TOP = 2
SPLIT = 2
GROUPS = 4
PREFIX = 2048
REQ_DEV = 4
SUF_MOST = 128
CAP = 40


epsilon = 1e-06


def spread(shard, axis, root):
    mine = lax.axis_index(axis) == root
    return lax.psum(jnp.where(mine, shard, jnp.zeros_like(shard)), axis)


def norm_rows(values, gain):
    squares = jnp.sum(values * values, axis=1)
    return values * lax.rsqrt(squares / values.shape[1] + epsilon)[:, None] * gain


def request_context(query_all, key_all, value_all, prefix_kv, start, length, window):
    row_count = query_all.shape[0]
    first = jnp.minimum(start, row_count - window)
    query_win = lax.dynamic_slice_in_dim(query_all, first, window, 0)
    key_win = lax.dynamic_slice_in_dim(key_all, first, window, 0)
    value_win = lax.dynamic_slice_in_dim(value_all, first, window, 0)
    keys = jnp.concatenate([prefix_kv[:, 0], key_win], axis=0)
    values = jnp.concatenate([prefix_kv[:, 1], value_win], axis=0)
    scores = jnp.einsum(
        "qhd,khd->hqk", query_win, keys, preferred_element_type=jnp.float32
    ) / math.sqrt(query_all.shape[2])
    positions = first + jnp.arange(window, dtype=jnp.int32)
    suffix_ok = (positions[None, :] <= positions[:, None]) & (positions[None, :] >= start)
    allowed = jnp.concatenate([jnp.ones((window, prefix_kv.shape[0]), bool), suffix_ok], axis=1)
    scores = jnp.where(allowed[None], scores, -1e30)
    highest = jnp.max(scores, axis=-1, keepdims=True)
    weight = jnp.exp(scores - highest)
    totals = jnp.sum(weight, axis=-1)
    context = jnp.einsum(
        "hqk,khd->qhd", weight.astype(jnp.bfloat16), values, preferred_element_type=jnp.float32
    )
    context = context / jnp.transpose(totals)[:, :, None]
    inside = (positions >= start) & (positions < start + length)
    context = context * inside[:, None, None].astype(jnp.float32)
    placed = jnp.zeros((row_count,) + context.shape[1:], jnp.float32)
    return lax.dynamic_update_slice_in_dim(placed, context, first, 0)


def attention_kernel(
    group_ref, start_ref, length_ref, query_ref, key_ref, value_ref, prefix_ref, out_ref
):
    request = pl.program_id(0)

    @pl.when(request == 0)
    def _():
        out_ref[...] = jnp.zeros_like(out_ref)

    start = start_ref[request]
    stop = start + length_ref[request]
    rows, width = query_ref.shape
    row_ids = lax.broadcasted_iota(jnp.int32, (rows, rows), 0)
    col_ids = lax.broadcasted_iota(jnp.int32, (rows, rows), 1)
    suffix_ok = (col_ids <= row_ids) & (col_ids >= start)
    lane_head = lax.broadcasted_iota(jnp.int32, (1, width), 1) // HEAD_DIM
    query = query_ref[...]
    keys = key_ref[...]
    values = value_ref[...]
    prefix_keys = prefix_ref[0, 0]
    prefix_values = prefix_ref[0, 1]
    scale = 1.0 / math.sqrt(HEAD_DIM)
    contract = (((1,), (1,)), ((), ()))
    context = jnp.zeros((rows, width), jnp.float32)
    for head in range(width // HEAD_DIM):
        in_head = lane_head == head
        query_h = jnp.where(in_head, query, jnp.zeros_like(query))
        score_pre = lax.dot_general(
            query_h, prefix_keys, contract, preferred_element_type=jnp.float32
        ) * scale
        score_suf = lax.dot_general(
            query_h, keys, contract, preferred_element_type=jnp.float32
        ) * scale
        score_suf = jnp.where(suffix_ok, score_suf, -1e30)
        highest = jnp.maximum(
            jnp.max(score_pre, axis=1, keepdims=True), jnp.max(score_suf, axis=1, keepdims=True)
        )
        weight_pre = jnp.exp(score_pre - highest)
        weight_suf = jnp.exp(score_suf - highest)
        totals = jnp.sum(weight_pre, axis=1, keepdims=True) + jnp.sum(
            weight_suf, axis=1, keepdims=True
        )
        mixed = jnp.dot(
            weight_pre.astype(jnp.bfloat16), prefix_values, preferred_element_type=jnp.float32
        ) + jnp.dot(weight_suf.astype(jnp.bfloat16), values, preferred_element_type=jnp.float32)
        context = context + jnp.where(in_head, mixed / totals, 0.0)
    row_in = lax.broadcasted_iota(jnp.int32, (rows, 1), 0)
    inside = (row_in >= start) & (row_in < stop)
    out_ref[...] = jnp.where(inside, context.astype(out_ref.dtype), out_ref[...])


def attention(query, keys, values, prefix, block_groups, starts, block_lengths, interpret=False):
    rows, width = query.shape
    slots = prefix.shape[0]
    full = lambda i, g, s, n: (0, 0)
    grid_spec = pltpu.PrefetchScalarGridSpec(
        num_scalar_prefetch=3,
        grid=(block_groups.shape[0],),
        in_specs=[
            pl.BlockSpec((rows, width), full),
            pl.BlockSpec((rows, width), full),
            pl.BlockSpec((rows, width), full),
            pl.BlockSpec((1, 2, PREFIX, width), lambda i, g, s, n: (g[i], 0, 0, 0)),
        ],
        out_specs=pl.BlockSpec((rows, width), full),
    )
    flops = 4 * 2 * 2 * rows * (PREFIX + rows) * width * block_groups.shape[0]
    return pl.pallas_call(
        attention_kernel,
        grid_spec=grid_spec,
        out_shape=jax.ShapeDtypeStruct((rows, width), jnp.bfloat16),
        compiler_params=pltpu.CompilerParams(dimension_semantics=("arbitrary",)),
        interpret=interpret,
        cost_estimate=pl.CostEstimate(
            flops=flops,
            transcendentals=4 * rows * (PREFIX + rows) * block_groups.shape[0],
            bytes_accessed=slots * 2 * PREFIX * width * 2 + 4 * rows * width * 2,
        ),
    )(
        jnp.clip(block_groups, 0, slots - 1),
        starts,
        block_lengths,
        query,
        keys,
        values,
        prefix,
    )


def slot_ranks(identity, experts):
    flat_ids = identity.reshape(-1)
    hits = (flat_ids[:, None] == jnp.arange(experts, dtype=jnp.int32)[None, :]).astype(jnp.int32)
    before = jnp.cumsum(hits, axis=0) - hits
    return (flat_ids, jnp.sum(before * hits, axis=1))


def slot_table(flat_ids, ranks, capacity, experts, row_count, topk):
    kept = ranks < capacity
    target = jnp.where(kept, flat_ids * capacity + ranks, experts * capacity)
    source = jnp.arange(flat_ids.shape[0], dtype=jnp.int32) // topk
    table = (
        jnp.full((experts * capacity,), row_count, jnp.int32).at[target].set(source, mode="drop")
    )
    return (kept, table)


def expert_apply(slots, weight_in, weight_down):
    joined = jnp.einsum("slcd,ldgh->slcgh", slots, weight_in, preferred_element_type=jnp.float32)
    units = (jax.nn.gelu(joined[:, :, :, 0], approximate=True) * joined[:, :, :, 1]).astype(
        jnp.bfloat16
    )
    return jnp.einsum("slch,lhd->slcd", units, weight_down, preferred_element_type=jnp.float32)


def shards(
    tokens,
    lengths,
    groups,
    owners,
    prefix_cache,
    attn_gain,
    w_qkv,
    w_out,
    moe_gain,
    w_router,
    expert_ids,
    w_in,
    w_down,
):
    rows_whole = lax.all_gather(tokens, "exp", axis=1, tiled=True)
    row_count = rows_whole.shape[0]
    full_width = rows_whole.shape[1]
    quarter = tokens.shape[1]
    local_heads = quarter // HEAD_DIM
    x_attn = norm_rows(rows_whole.astype(jnp.float32), attn_gain).astype(jnp.bfloat16)
    qkv = jnp.dot(
        x_attn, w_qkv.reshape(full_width, 3 * quarter), preferred_element_type=jnp.float32
    )
    qkv = qkv.astype(jnp.bfloat16).reshape(row_count, 3, quarter)
    suffix_kv = jnp.stack([qkv[:, 1], qkv[:, 2]], axis=1)
    own_slot = prefix_cache[0]
    block_lengths = lengths[0]
    block_groups = groups[0]
    starts = jnp.cumsum(block_lengths) - block_lengths
    req_total = lax.axis_size("req")
    pieces = own_slot.reshape(req_total, PREFIX // req_total, 2, quarter)
    pieces = lax.all_to_all(pieces, "req", split_axis=0, concat_axis=0, tiled=True)
    owned = jnp.take(pieces, owners, axis=0)
    cached = lax.all_gather(owned, "req", axis=1, tiled=True)
    cached = jnp.transpose(cached, (0, 2, 1, 3))
    context = attention(
        qkv[:, 0], qkv[:, 1], qkv[:, 2], cached, block_groups, starts, block_lengths
    )
    partial_attn = jnp.dot(context, w_out, preferred_element_type=jnp.float32)
    resid = tokens.astype(jnp.float32) + lax.psum_scatter(
        partial_attn.astype(jnp.bfloat16), "exp", scatter_dimension=1, tiled=True
    ).astype(jnp.float32)
    squares = lax.psum(jnp.sum(resid * resid, axis=1), "exp")
    column_start = lax.axis_index("exp") * quarter
    gain_part = lax.dynamic_slice_in_dim(moe_gain, column_start, quarter, 0)
    x_part = (resid * lax.rsqrt(squares / full_width + epsilon)[:, None] * gain_part).astype(
        jnp.bfloat16
    )
    x_source = lax.all_gather(x_part, "exp", axis=1, tiled=True)
    logits = jnp.dot(x_source, w_router, preferred_element_type=jnp.float32)
    gates = jax.nn.sigmoid(jnp.take_along_axis(logits, expert_ids, axis=1)).reshape(-1)
    flat_ids, ranks = slot_ranks(expert_ids, EXPERTS)
    kept, table = slot_table(flat_ids, ranks, CAP, EXPERTS, row_count, TOP)
    columns = x_source.shape[1]
    padded = jnp.concatenate([x_source, jnp.zeros((1, columns), x_source.dtype)], axis=0)
    picked = padded[table].reshape(EXPERTS, 1, CAP, columns)
    local_rows = EXPERTS * SPLIT // req_total
    outgoing_rows = jnp.broadcast_to(picked, (EXPERTS, SPLIT, CAP, columns)).reshape(
        req_total, local_rows, CAP, columns
    )
    partial_out = expert_apply(
        lax.all_to_all(outgoing_rows, "req", split_axis=0, concat_axis=0, tiled=True), w_in, w_down
    )
    returned = lax.all_to_all(
        partial_out.astype(jnp.bfloat16), "req", split_axis=0, concat_axis=0, tiled=True
    ).astype(partial_out.dtype)
    out_columns = returned.shape[3]
    summed = jnp.sum(returned.reshape(EXPERTS, SPLIT, CAP, out_columns), axis=1).reshape(
        EXPERTS * CAP, out_columns
    )
    source = flat_ids * CAP + jnp.minimum(ranks, CAP - 1)
    chosen = summed[source].reshape(row_count, TOP, out_columns)
    scale = jnp.where(kept, gates, 0.0).reshape(row_count, TOP)
    mixture = jnp.sum(chosen * scale[:, :, None], axis=1)
    moe_part = lax.psum_scatter(
        mixture.astype(jnp.bfloat16), "exp", scatter_dimension=1, tiled=True
    ).astype(jnp.float32)
    hidden_out = (resid + moe_part).astype(jnp.bfloat16)
    return (hidden_out, suffix_kv)


def solution(mesh):
    return jax.shard_map(
        shards,
        mesh=mesh,
        in_specs=(
            P("req", "exp"),
            P("req", None),
            P("req", None),
            P(),
            P("req", None, None, "exp"),
            P(),
            P(None, None, "exp"),
            P("exp", None),
            P(),
            P(),
            P("req", None),
            P("req", None, None, "exp"),
            P("req", "exp", None),
        ),
        out_specs=(P("req", "exp"), P("req", None, "exp")),
        check_vma=False,
    )
```

```python
import math

import jax
import jax.numpy as jnp
from jax import lax
from jax.sharding import PartitionSpec as P
from jax.experimental import pallas as pl
from jax.experimental.pallas import tpu as pltpu

HEAD_DIM = 64
EXPERTS = 16
TOP = 2
SPLIT = 2
GROUPS = 4
PREFIX = 2048
REQ_DEV = 4
SUF_MOST = 128
CAP = 40


epsilon = 1e-06


def spread(shard, axis, root):
    mine = lax.axis_index(axis) == root
    return lax.psum(jnp.where(mine, shard, jnp.zeros_like(shard)), axis)


def norm_rows(values, gain):
    squares = jnp.sum(values * values, axis=1)
    return values * lax.rsqrt(squares / values.shape[1] + epsilon)[:, None] * gain


def request_context(query_all, key_all, value_all, prefix_kv, start, length, window):
    row_count = query_all.shape[0]
    first = jnp.minimum(start, row_count - window)
    query_win = lax.dynamic_slice_in_dim(query_all, first, window, 0)
    key_win = lax.dynamic_slice_in_dim(key_all, first, window, 0)
    value_win = lax.dynamic_slice_in_dim(value_all, first, window, 0)
    keys = jnp.concatenate([prefix_kv[:, 0], key_win], axis=0)
    values = jnp.concatenate([prefix_kv[:, 1], value_win], axis=0)
    scores = jnp.einsum(
        "qhd,khd->hqk", query_win, keys, preferred_element_type=jnp.float32
    ) / math.sqrt(query_all.shape[2])
    positions = first + jnp.arange(window, dtype=jnp.int32)
    suffix_ok = (positions[None, :] <= positions[:, None]) & (positions[None, :] >= start)
    allowed = jnp.concatenate([jnp.ones((window, prefix_kv.shape[0]), bool), suffix_ok], axis=1)
    scores = jnp.where(allowed[None], scores, -1e30)
    highest = jnp.max(scores, axis=-1, keepdims=True)
    weight = jnp.exp(scores - highest)
    totals = jnp.sum(weight, axis=-1)
    context = jnp.einsum(
        "hqk,khd->qhd", weight.astype(jnp.bfloat16), values, preferred_element_type=jnp.float32
    )
    context = context / jnp.transpose(totals)[:, :, None]
    inside = (positions >= start) & (positions < start + length)
    context = context * inside[:, None, None].astype(jnp.float32)
    placed = jnp.zeros((row_count,) + context.shape[1:], jnp.float32)
    return lax.dynamic_update_slice_in_dim(placed, context, first, 0)


def attention_kernel(
    group_ref, start_ref, length_ref, query_ref, key_ref, value_ref, prefix_ref, out_ref
):
    request = pl.program_id(0)

    @pl.when(request == 0)
    def _():
        out_ref[...] = jnp.zeros_like(out_ref)

    start = start_ref[request]
    stop = start + length_ref[request]
    rows, width = query_ref.shape
    row_ids = lax.broadcasted_iota(jnp.int32, (rows, rows), 0)
    col_ids = lax.broadcasted_iota(jnp.int32, (rows, rows), 1)
    suffix_ok = (col_ids <= row_ids) & (col_ids >= start)
    lane_head = lax.broadcasted_iota(jnp.int32, (1, width), 1) // HEAD_DIM
    query = query_ref[...]
    keys = key_ref[...]
    values = value_ref[...]
    prefix_keys = prefix_ref[0, 0]
    prefix_values = prefix_ref[0, 1]
    scale = 1.0 / math.sqrt(HEAD_DIM)
    contract = (((1,), (1,)), ((), ()))
    context = jnp.zeros((rows, width), jnp.float32)
    for head in range(width // HEAD_DIM):
        in_head = lane_head == head
        query_h = jnp.where(in_head, query, jnp.zeros_like(query))
        score_pre = lax.dot_general(
            query_h, prefix_keys, contract, preferred_element_type=jnp.float32
        ) * scale
        score_suf = lax.dot_general(
            query_h, keys, contract, preferred_element_type=jnp.float32
        ) * scale
        score_suf = jnp.where(suffix_ok, score_suf, -1e30)
        highest = jnp.maximum(
            jnp.max(score_pre, axis=1, keepdims=True), jnp.max(score_suf, axis=1, keepdims=True)
        )
        weight_pre = jnp.exp(score_pre - highest)
        weight_suf = jnp.exp(score_suf - highest)
        totals = jnp.sum(weight_pre, axis=1, keepdims=True) + jnp.sum(
            weight_suf, axis=1, keepdims=True
        )
        mixed = jnp.dot(
            weight_pre.astype(jnp.bfloat16), prefix_values, preferred_element_type=jnp.float32
        ) + jnp.dot(weight_suf.astype(jnp.bfloat16), values, preferred_element_type=jnp.float32)
        context = context + jnp.where(in_head, mixed / totals, 0.0)
    row_in = lax.broadcasted_iota(jnp.int32, (rows, 1), 0)
    inside = (row_in >= start) & (row_in < stop)
    out_ref[...] = jnp.where(inside, context.astype(out_ref.dtype), out_ref[...])


def attention(query, keys, values, prefix, block_groups, starts, block_lengths, interpret=False):
    rows, width = query.shape
    slots = prefix.shape[0]
    full = lambda i, g, s, n: (0, 0)
    grid_spec = pltpu.PrefetchScalarGridSpec(
        num_scalar_prefetch=3,
        grid=(block_groups.shape[0],),
        in_specs=[
            pl.BlockSpec((rows, width), full),
            pl.BlockSpec((rows, width), full),
            pl.BlockSpec((rows, width), full),
            pl.BlockSpec((1, 2, PREFIX, width), lambda i, g, s, n: (g[i], 0, 0, 0)),
        ],
        out_specs=pl.BlockSpec((rows, width), full),
    )
    flops = 4 * 2 * 2 * rows * (PREFIX + rows) * width * block_groups.shape[0]
    return pl.pallas_call(
        attention_kernel,
        grid_spec=grid_spec,
        out_shape=jax.ShapeDtypeStruct((rows, width), jnp.bfloat16),
        compiler_params=pltpu.CompilerParams(dimension_semantics=("arbitrary",)),
        interpret=interpret,
        cost_estimate=pl.CostEstimate(
            flops=flops,
            transcendentals=4 * rows * (PREFIX + rows) * block_groups.shape[0],
            bytes_accessed=slots * 2 * PREFIX * width * 2 + 4 * rows * width * 2,
        ),
    )(
        jnp.clip(block_groups, 0, slots - 1),
        starts,
        block_lengths,
        query,
        keys,
        values,
        prefix,
    )


def slot_ranks(identity, experts):
    flat_ids = identity.reshape(-1)
    hits = (flat_ids[:, None] == jnp.arange(experts, dtype=jnp.int32)[None, :]).astype(jnp.int32)
    before = jnp.cumsum(hits, axis=0) - hits
    return (flat_ids, jnp.sum(before * hits, axis=1))


def slot_table(flat_ids, ranks, capacity, experts, row_count, topk):
    kept = ranks < capacity
    target = jnp.where(kept, flat_ids * capacity + ranks, experts * capacity)
    source = jnp.arange(flat_ids.shape[0], dtype=jnp.int32) // topk
    table = (
        jnp.full((experts * capacity,), row_count, jnp.int32).at[target].set(source, mode="drop")
    )
    return (kept, table)


def expert_apply(slots, weight_in, weight_down):
    joined = jnp.einsum("slcd,ldgh->slcgh", slots, weight_in, preferred_element_type=jnp.float32)
    units = (jax.nn.gelu(joined[:, :, :, 0], approximate=True) * joined[:, :, :, 1]).astype(
        jnp.bfloat16
    )
    return jnp.einsum("slch,lhd->slcd", units, weight_down, preferred_element_type=jnp.float32)


def shards(
    tokens,
    lengths,
    groups,
    owners,
    prefix_cache,
    attn_gain,
    w_qkv,
    w_out,
    moe_gain,
    w_router,
    expert_ids,
    w_in,
    w_down,
):
    rows_whole = lax.all_gather(tokens, "exp", axis=1, tiled=True)
    row_count = rows_whole.shape[0]
    full_width = rows_whole.shape[1]
    quarter = tokens.shape[1]
    local_heads = quarter // HEAD_DIM
    x_attn = norm_rows(rows_whole.astype(jnp.float32), attn_gain).astype(jnp.bfloat16)
    qkv = jnp.dot(
        x_attn, w_qkv.reshape(full_width, 3 * quarter), preferred_element_type=jnp.float32
    )
    qkv = qkv.astype(jnp.bfloat16).reshape(row_count, 3, quarter)
    suffix_kv = jnp.stack([qkv[:, 1], qkv[:, 2]], axis=1)
    own_slot = prefix_cache[0]
    block_lengths = lengths[0]
    block_groups = groups[0]
    starts = jnp.cumsum(block_lengths) - block_lengths
    req_total = lax.axis_size("req")
    pieces = own_slot.reshape(req_total, PREFIX // req_total, 2, quarter)
    pieces = lax.all_to_all(pieces, "req", split_axis=0, concat_axis=0, tiled=True)
    owned = jnp.take(pieces, owners, axis=0)
    cached = lax.all_gather(owned, "req", axis=1, tiled=True)
    cached = jnp.transpose(cached, (0, 2, 1, 3))
    context = attention(
        qkv[:, 0], qkv[:, 1], qkv[:, 2], cached, block_groups, starts, block_lengths
    )
    partial_attn = jnp.dot(context, w_out, preferred_element_type=jnp.float32)
    resid = tokens.astype(jnp.float32) + lax.psum_scatter(
        partial_attn.astype(jnp.bfloat16), "exp", scatter_dimension=1, tiled=True
    ).astype(jnp.float32)
    squares = lax.psum(jnp.sum(resid * resid, axis=1), "exp")
    column_start = lax.axis_index("exp") * quarter
    gain_part = lax.dynamic_slice_in_dim(moe_gain, column_start, quarter, 0)
    x_part = (resid * lax.rsqrt(squares / full_width + epsilon)[:, None] * gain_part).astype(
        jnp.bfloat16
    )
    x_source = lax.all_gather(x_part, "exp", axis=1, tiled=True)
    logits = jnp.dot(x_source, w_router, preferred_element_type=jnp.float32)
    gates = jax.nn.sigmoid(jnp.take_along_axis(logits, expert_ids, axis=1)).reshape(-1)
    flat_ids, ranks = slot_ranks(expert_ids, EXPERTS)
    kept, table = slot_table(flat_ids, ranks, CAP, EXPERTS, row_count, TOP)
    columns = x_source.shape[1]
    padded = jnp.concatenate([x_source, jnp.zeros((1, columns), x_source.dtype)], axis=0)
    picked = padded[table].reshape(EXPERTS, 1, CAP, columns)
    local_rows = EXPERTS * SPLIT // req_total
    outgoing_rows = jnp.broadcast_to(picked, (EXPERTS, SPLIT, CAP, columns)).reshape(
        req_total, local_rows, CAP, columns
    )
    partial_out = expert_apply(
        lax.all_to_all(outgoing_rows, "req", split_axis=0, concat_axis=0, tiled=True), w_in, w_down
    )
    returned = lax.all_to_all(
        partial_out.astype(jnp.bfloat16), "req", split_axis=0, concat_axis=0, tiled=True
    ).astype(partial_out.dtype)
    block_count, _, _, out_columns = returned.shape
    pair_column = flat_ids * (SPLIT * CAP) + jnp.minimum(ranks, CAP - 1)
    pair_scale = jnp.where(kept, gates, 0.0)
    columns_all = lax.broadcasted_iota(jnp.int32, (row_count * TOP, block_count * CAP), 1)
    offset = columns_all - pair_column[:, None]
    hit = (offset == 0) | (offset == CAP)
    selection = jnp.where(hit, pair_scale[:, None], 0.0).reshape(row_count, TOP, -1).sum(axis=1)
    mixture = jnp.dot(
        selection,
        returned.reshape(block_count * CAP, out_columns).astype(jnp.float32),
        precision=lax.Precision.HIGHEST,
        preferred_element_type=jnp.float32,
    )
    moe_part = lax.psum_scatter(
        mixture.astype(jnp.bfloat16), "exp", scatter_dimension=1, tiled=True
    ).astype(jnp.float32)
    hidden_out = (resid + moe_part).astype(jnp.bfloat16)
    return (hidden_out, suffix_kv)


def solution(mesh):
    return jax.shard_map(
        shards,
        mesh=mesh,
        in_specs=(
            P("req", "exp"),
            P("req", None),
            P("req", None),
            P(),
            P("req", None, None, "exp"),
            P(),
            P(None, None, "exp"),
            P("exp", None),
            P(),
            P(),
            P("req", None),
            P("req", None, None, "exp"),
            P("req", "exp", None),
        ),
        out_specs=(P("req", "exp"), P("req", None, "exp")),
        check_vma=False,
    )
```

```python
import math

import jax
import jax.numpy as jnp
from jax import lax
from jax.sharding import PartitionSpec as P
from jax.experimental import pallas as pl
from jax.experimental.pallas import tpu as pltpu

HEAD_DIM = 64
EXPERTS = 16
TOP = 2
SPLIT = 2
GROUPS = 4
PREFIX = 2048
REQ_DEV = 4
SUF_MOST = 128
CAP = 40


epsilon = 1e-06


def spread(shard, axis, root):
    mine = lax.axis_index(axis) == root
    return lax.psum(jnp.where(mine, shard, jnp.zeros_like(shard)), axis)


def norm_rows(values, gain):
    squares = jnp.sum(values * values, axis=1)
    return values * lax.rsqrt(squares / values.shape[1] + epsilon)[:, None] * gain


def request_context(query_all, key_all, value_all, prefix_kv, start, length, window):
    row_count = query_all.shape[0]
    first = jnp.minimum(start, row_count - window)
    query_win = lax.dynamic_slice_in_dim(query_all, first, window, 0)
    key_win = lax.dynamic_slice_in_dim(key_all, first, window, 0)
    value_win = lax.dynamic_slice_in_dim(value_all, first, window, 0)
    keys = jnp.concatenate([prefix_kv[:, 0], key_win], axis=0)
    values = jnp.concatenate([prefix_kv[:, 1], value_win], axis=0)
    scores = jnp.einsum(
        "qhd,khd->hqk", query_win, keys, preferred_element_type=jnp.float32
    ) / math.sqrt(query_all.shape[2])
    positions = first + jnp.arange(window, dtype=jnp.int32)
    suffix_ok = (positions[None, :] <= positions[:, None]) & (positions[None, :] >= start)
    allowed = jnp.concatenate([jnp.ones((window, prefix_kv.shape[0]), bool), suffix_ok], axis=1)
    scores = jnp.where(allowed[None], scores, -1e30)
    highest = jnp.max(scores, axis=-1, keepdims=True)
    weight = jnp.exp(scores - highest)
    totals = jnp.sum(weight, axis=-1)
    context = jnp.einsum(
        "hqk,khd->qhd", weight.astype(jnp.bfloat16), values, preferred_element_type=jnp.float32
    )
    context = context / jnp.transpose(totals)[:, :, None]
    inside = (positions >= start) & (positions < start + length)
    context = context * inside[:, None, None].astype(jnp.float32)
    placed = jnp.zeros((row_count,) + context.shape[1:], jnp.float32)
    return lax.dynamic_update_slice_in_dim(placed, context, first, 0)


def attention_kernel(
    group_ref, start_ref, length_ref, query_ref, key_ref, value_ref, prefix_ref, out_ref
):
    request = pl.program_id(0)

    @pl.when(request == 0)
    def _():
        out_ref[...] = jnp.zeros_like(out_ref)

    start = start_ref[request]
    stop = start + length_ref[request]
    rows, width = query_ref.shape
    row_ids = lax.broadcasted_iota(jnp.int32, (rows, rows), 0)
    col_ids = lax.broadcasted_iota(jnp.int32, (rows, rows), 1)
    suffix_ok = (col_ids <= row_ids) & (col_ids >= start)
    lane_head = lax.broadcasted_iota(jnp.int32, (1, width), 1) // HEAD_DIM
    query = query_ref[...]
    keys = key_ref[...]
    values = value_ref[...]
    prefix_keys = prefix_ref[0, 0]
    prefix_values = prefix_ref[0, 1]
    scale = 1.0 / math.sqrt(HEAD_DIM)
    contract = (((1,), (1,)), ((), ()))
    context = jnp.zeros((rows, width), jnp.float32)
    for head in range(width // HEAD_DIM):
        in_head = lane_head == head
        query_h = jnp.where(in_head, query, jnp.zeros_like(query))
        score_pre = lax.dot_general(
            query_h, prefix_keys, contract, preferred_element_type=jnp.float32
        ) * scale
        score_suf = lax.dot_general(
            query_h, keys, contract, preferred_element_type=jnp.float32
        ) * scale
        score_suf = jnp.where(suffix_ok, score_suf, -1e30)
        highest = jnp.maximum(
            jnp.max(score_pre, axis=1, keepdims=True), jnp.max(score_suf, axis=1, keepdims=True)
        )
        weight_pre = jnp.exp(score_pre - highest)
        weight_suf = jnp.exp(score_suf - highest)
        totals = jnp.sum(weight_pre, axis=1, keepdims=True) + jnp.sum(
            weight_suf, axis=1, keepdims=True
        )
        mixed = jnp.dot(
            weight_pre.astype(jnp.bfloat16), prefix_values, preferred_element_type=jnp.float32
        ) + jnp.dot(weight_suf.astype(jnp.bfloat16), values, preferred_element_type=jnp.float32)
        context = context + jnp.where(in_head, mixed / totals, 0.0)
    row_in = lax.broadcasted_iota(jnp.int32, (rows, 1), 0)
    inside = (row_in >= start) & (row_in < stop)
    out_ref[...] = jnp.where(inside, context.astype(out_ref.dtype), out_ref[...])


def attention(query, keys, values, prefix, block_groups, starts, block_lengths, interpret=False):
    rows, width = query.shape
    slots = prefix.shape[0]
    full = lambda i, g, s, n: (0, 0)
    grid_spec = pltpu.PrefetchScalarGridSpec(
        num_scalar_prefetch=3,
        grid=(block_groups.shape[0],),
        in_specs=[
            pl.BlockSpec((rows, width), full),
            pl.BlockSpec((rows, width), full),
            pl.BlockSpec((rows, width), full),
            pl.BlockSpec((1, 2, PREFIX, width), lambda i, g, s, n: (g[i], 0, 0, 0)),
        ],
        out_specs=pl.BlockSpec((rows, width), full),
    )
    flops = 4 * 2 * 2 * rows * (PREFIX + rows) * width * block_groups.shape[0]
    return pl.pallas_call(
        attention_kernel,
        grid_spec=grid_spec,
        out_shape=jax.ShapeDtypeStruct((rows, width), jnp.bfloat16),
        compiler_params=pltpu.CompilerParams(dimension_semantics=("arbitrary",)),
        interpret=interpret,
        cost_estimate=pl.CostEstimate(
            flops=flops,
            transcendentals=4 * rows * (PREFIX + rows) * block_groups.shape[0],
            bytes_accessed=slots * 2 * PREFIX * width * 2 + 4 * rows * width * 2,
        ),
    )(
        jnp.clip(block_groups, 0, slots - 1),
        starts,
        block_lengths,
        query,
        keys,
        values,
        prefix,
    )


def slot_ranks(identity, experts):
    flat_ids = identity.reshape(-1)
    hits = (flat_ids[:, None] == jnp.arange(experts, dtype=jnp.int32)[None, :]).astype(jnp.int32)
    before = jnp.cumsum(hits, axis=0) - hits
    return (flat_ids, jnp.sum(before * hits, axis=1))


def slot_table(flat_ids, ranks, capacity, experts, row_count, topk):
    kept = ranks < capacity
    target = jnp.where(kept, flat_ids * capacity + ranks, experts * capacity)
    source = jnp.arange(flat_ids.shape[0], dtype=jnp.int32) // topk
    table = (
        jnp.full((experts * capacity,), row_count, jnp.int32).at[target].set(source, mode="drop")
    )
    return (kept, table)


def expert_apply(slots, weight_in, weight_down):
    joined = jnp.einsum("slcd,ldgh->slcgh", slots, weight_in, preferred_element_type=jnp.float32)
    units = (jax.nn.gelu(joined[:, :, :, 0], approximate=True) * joined[:, :, :, 1]).astype(
        jnp.bfloat16
    )
    return jnp.einsum("slch,lhd->slcd", units, weight_down, preferred_element_type=jnp.float32)


def shards(
    tokens,
    lengths,
    groups,
    owners,
    prefix_cache,
    attn_gain,
    w_qkv,
    w_out,
    moe_gain,
    w_router,
    expert_ids,
    w_in,
    w_down,
):
    rows_whole = lax.all_gather(tokens, "exp", axis=1, tiled=True)
    row_count = rows_whole.shape[0]
    full_width = rows_whole.shape[1]
    quarter = tokens.shape[1]
    local_heads = quarter // HEAD_DIM
    x_attn = norm_rows(rows_whole.astype(jnp.float32), attn_gain).astype(jnp.bfloat16)
    qkv = jnp.dot(
        x_attn, w_qkv.reshape(full_width, 3 * quarter), preferred_element_type=jnp.float32
    )
    qkv = qkv.astype(jnp.bfloat16).reshape(row_count, 3, quarter)
    suffix_kv = jnp.stack([qkv[:, 1], qkv[:, 2]], axis=1)
    own_slot = prefix_cache[0]
    block_lengths = lengths[0]
    block_groups = groups[0]
    starts = jnp.cumsum(block_lengths) - block_lengths
    req_total = lax.axis_size("req")
    pieces = own_slot.reshape(req_total, PREFIX // req_total, 2, quarter)
    pieces = lax.all_to_all(pieces, "req", split_axis=0, concat_axis=0, tiled=True)
    owned = jnp.take(pieces, owners, axis=0)
    cached = lax.all_gather(owned, "req", axis=1, tiled=True)
    cached = jnp.transpose(cached, (0, 2, 1, 3))
    context = attention(
        qkv[:, 0], qkv[:, 1], qkv[:, 2], cached, block_groups, starts, block_lengths
    )
    context_full = lax.all_gather(context, "exp", axis=1, tiled=True)
    w_out_full = lax.all_gather(w_out, "exp", axis=0, tiled=True)
    attn_full = jnp.dot(context_full, w_out_full, preferred_element_type=jnp.float32)
    resid_full = rows_whole.astype(jnp.float32) + attn_full
    x_source = norm_rows(resid_full, moe_gain).astype(jnp.bfloat16)
    column_start = lax.axis_index("exp") * quarter
    resid = lax.dynamic_slice_in_dim(resid_full, column_start, quarter, 1)
    logits = jnp.dot(x_source, w_router, preferred_element_type=jnp.float32)
    gates = jax.nn.sigmoid(jnp.take_along_axis(logits, expert_ids, axis=1)).reshape(-1)
    flat_ids, ranks = slot_ranks(expert_ids, EXPERTS)
    kept, table = slot_table(flat_ids, ranks, CAP, EXPERTS, row_count, TOP)
    columns = x_source.shape[1]
    padded = jnp.concatenate([x_source, jnp.zeros((1, columns), x_source.dtype)], axis=0)
    picked = padded[table].reshape(EXPERTS, 1, CAP, columns)
    local_rows = EXPERTS * SPLIT // req_total
    outgoing_rows = jnp.broadcast_to(picked, (EXPERTS, SPLIT, CAP, columns)).reshape(
        req_total, local_rows, CAP, columns
    )
    partial_out = expert_apply(
        lax.all_to_all(outgoing_rows, "req", split_axis=0, concat_axis=0, tiled=True), w_in, w_down
    )
    returned = lax.all_to_all(
        partial_out.astype(jnp.bfloat16), "req", split_axis=0, concat_axis=0, tiled=True
    ).astype(partial_out.dtype)
    block_count, _, _, out_columns = returned.shape
    pair_column = flat_ids * (SPLIT * CAP) + jnp.minimum(ranks, CAP - 1)
    pair_scale = jnp.where(kept, gates, 0.0)
    columns_all = lax.broadcasted_iota(jnp.int32, (row_count * TOP, block_count * CAP), 1)
    offset = columns_all - pair_column[:, None]
    hit = (offset == 0) | (offset == CAP)
    selection = jnp.where(hit, pair_scale[:, None], 0.0).reshape(row_count, TOP, -1).sum(axis=1)
    mixture = jnp.dot(
        selection,
        returned.reshape(block_count * CAP, out_columns).astype(jnp.float32),
        precision=lax.Precision.HIGHEST,
        preferred_element_type=jnp.float32,
    )
    moe_part = lax.psum_scatter(
        mixture.astype(jnp.bfloat16), "exp", scatter_dimension=1, tiled=True
    ).astype(jnp.float32)
    hidden_out = (resid + moe_part).astype(jnp.bfloat16)
    return (hidden_out, suffix_kv)


def solution(mesh):
    return jax.shard_map(
        shards,
        mesh=mesh,
        in_specs=(
            P("req", "exp"),
            P("req", None),
            P("req", None),
            P(),
            P("req", None, None, "exp"),
            P(),
            P(None, None, "exp"),
            P("exp", None),
            P(),
            P(),
            P("req", None),
            P("req", None, None, "exp"),
            P("req", "exp", None),
        ),
        out_specs=(P("req", "exp"), P("req", None, "exp")),
        check_vma=False,
    )
```

```python
import math

import jax
import jax.numpy as jnp
from jax import lax
from jax.sharding import PartitionSpec as P
from jax.experimental import pallas as pl
from jax.experimental.pallas import tpu as pltpu

HEAD_DIM = 64
EXPERTS = 16
TOP = 2
SPLIT = 2
GROUPS = 4
PREFIX = 2048
REQ_DEV = 4
SUF_MOST = 128
CAP = 40


epsilon = 1e-06


def spread(shard, axis, root):
    mine = lax.axis_index(axis) == root
    return lax.psum(jnp.where(mine, shard, jnp.zeros_like(shard)), axis)


def norm_rows(values, gain):
    squares = jnp.sum(values * values, axis=1)
    return values * lax.rsqrt(squares / values.shape[1] + epsilon)[:, None] * gain


def request_context(query_all, key_all, value_all, prefix_kv, start, length, window):
    row_count = query_all.shape[0]
    first = jnp.minimum(start, row_count - window)
    query_win = lax.dynamic_slice_in_dim(query_all, first, window, 0)
    key_win = lax.dynamic_slice_in_dim(key_all, first, window, 0)
    value_win = lax.dynamic_slice_in_dim(value_all, first, window, 0)
    keys = jnp.concatenate([prefix_kv[:, 0], key_win], axis=0)
    values = jnp.concatenate([prefix_kv[:, 1], value_win], axis=0)
    scores = jnp.einsum(
        "qhd,khd->hqk", query_win, keys, preferred_element_type=jnp.float32
    ) / math.sqrt(query_all.shape[2])
    positions = first + jnp.arange(window, dtype=jnp.int32)
    suffix_ok = (positions[None, :] <= positions[:, None]) & (positions[None, :] >= start)
    allowed = jnp.concatenate([jnp.ones((window, prefix_kv.shape[0]), bool), suffix_ok], axis=1)
    scores = jnp.where(allowed[None], scores, -1e30)
    highest = jnp.max(scores, axis=-1, keepdims=True)
    weight = jnp.exp(scores - highest)
    totals = jnp.sum(weight, axis=-1)
    context = jnp.einsum(
        "hqk,khd->qhd", weight.astype(jnp.bfloat16), values, preferred_element_type=jnp.float32
    )
    context = context / jnp.transpose(totals)[:, :, None]
    inside = (positions >= start) & (positions < start + length)
    context = context * inside[:, None, None].astype(jnp.float32)
    placed = jnp.zeros((row_count,) + context.shape[1:], jnp.float32)
    return lax.dynamic_update_slice_in_dim(placed, context, first, 0)


def attention_kernel(
    group_ref, start_ref, length_ref, query_ref, key_ref, value_ref, prefix_ref, out_ref
):
    request = pl.program_id(0)

    @pl.when(request == 0)
    def _():
        out_ref[...] = jnp.zeros_like(out_ref)

    start = start_ref[request]
    stop = start + length_ref[request]
    rows, width = query_ref.shape
    row_ids = lax.broadcasted_iota(jnp.int32, (rows, rows), 0)
    col_ids = lax.broadcasted_iota(jnp.int32, (rows, rows), 1)
    suffix_ok = (col_ids <= row_ids) & (col_ids >= start)
    lane_head = lax.broadcasted_iota(jnp.int32, (1, width), 1) // HEAD_DIM
    query = query_ref[...]
    keys = key_ref[...]
    values = value_ref[...]
    prefix_keys = prefix_ref[0, 0]
    prefix_values = prefix_ref[0, 1]
    scale = 1.0 / math.sqrt(HEAD_DIM)
    contract = (((1,), (1,)), ((), ()))
    context = jnp.zeros((rows, width), jnp.float32)
    for head in range(width // HEAD_DIM):
        in_head = lane_head == head
        query_h = jnp.where(in_head, query, jnp.zeros_like(query))
        score_pre = lax.dot_general(
            query_h, prefix_keys, contract, preferred_element_type=jnp.float32
        ) * scale
        score_suf = lax.dot_general(
            query_h, keys, contract, preferred_element_type=jnp.float32
        ) * scale
        score_suf = jnp.where(suffix_ok, score_suf, -1e30)
        highest = jnp.maximum(
            jnp.max(score_pre, axis=1, keepdims=True), jnp.max(score_suf, axis=1, keepdims=True)
        )
        weight_pre = jnp.exp(score_pre - highest)
        weight_suf = jnp.exp(score_suf - highest)
        totals = jnp.sum(weight_pre, axis=1, keepdims=True) + jnp.sum(
            weight_suf, axis=1, keepdims=True
        )
        mixed = jnp.dot(
            weight_pre.astype(jnp.bfloat16), prefix_values, preferred_element_type=jnp.float32
        ) + jnp.dot(weight_suf.astype(jnp.bfloat16), values, preferred_element_type=jnp.float32)
        context = context + jnp.where(in_head, mixed / totals, 0.0)
    row_in = lax.broadcasted_iota(jnp.int32, (rows, 1), 0)
    inside = (row_in >= start) & (row_in < stop)
    out_ref[...] = jnp.where(inside, context.astype(out_ref.dtype), out_ref[...])


def attention(query, keys, values, prefix, block_groups, starts, block_lengths, interpret=False):
    rows, width = query.shape
    slots = prefix.shape[0]
    full = lambda i, g, s, n: (0, 0)
    grid_spec = pltpu.PrefetchScalarGridSpec(
        num_scalar_prefetch=3,
        grid=(block_groups.shape[0],),
        in_specs=[
            pl.BlockSpec((rows, width), full),
            pl.BlockSpec((rows, width), full),
            pl.BlockSpec((rows, width), full),
            pl.BlockSpec((1, 2, PREFIX, width), lambda i, g, s, n: (g[i], 0, 0, 0)),
        ],
        out_specs=pl.BlockSpec((rows, width), full),
    )
    flops = 4 * 2 * 2 * rows * (PREFIX + rows) * width * block_groups.shape[0]
    return pl.pallas_call(
        attention_kernel,
        grid_spec=grid_spec,
        out_shape=jax.ShapeDtypeStruct((rows, width), jnp.bfloat16),
        compiler_params=pltpu.CompilerParams(dimension_semantics=("arbitrary",)),
        interpret=interpret,
        cost_estimate=pl.CostEstimate(
            flops=flops,
            transcendentals=4 * rows * (PREFIX + rows) * block_groups.shape[0],
            bytes_accessed=slots * 2 * PREFIX * width * 2 + 4 * rows * width * 2,
        ),
    )(
        jnp.clip(block_groups, 0, slots - 1),
        starts,
        block_lengths,
        query,
        keys,
        values,
        prefix,
    )


def slot_ranks(identity, experts):
    flat_ids = identity.reshape(-1)
    hits = (flat_ids[:, None] == jnp.arange(experts, dtype=jnp.int32)[None, :]).astype(jnp.int32)
    before = jnp.cumsum(hits, axis=0) - hits
    return (flat_ids, jnp.sum(before * hits, axis=1))


def slot_table(flat_ids, ranks, capacity, experts, row_count, topk):
    kept = ranks < capacity
    target = jnp.where(kept, flat_ids * capacity + ranks, experts * capacity)
    source = jnp.arange(flat_ids.shape[0], dtype=jnp.int32) // topk
    table = (
        jnp.full((experts * capacity,), row_count, jnp.int32).at[target].set(source, mode="drop")
    )
    return (kept, table)


def expert_apply(slots, weight_in, weight_down):
    joined = jnp.einsum("slcd,ldgh->slcgh", slots, weight_in, preferred_element_type=jnp.float32)
    units = (jax.nn.gelu(joined[:, :, :, 0], approximate=True) * joined[:, :, :, 1]).astype(
        jnp.bfloat16
    )
    return jnp.einsum("slch,lhd->slcd", units, weight_down, preferred_element_type=jnp.float32)


def shards(
    tokens,
    lengths,
    groups,
    owners,
    prefix_cache,
    attn_gain,
    w_qkv,
    w_out,
    moe_gain,
    w_router,
    expert_ids,
    w_in,
    w_down,
):
    rows_whole = lax.all_gather(tokens, "exp", axis=1, tiled=True)
    row_count = rows_whole.shape[0]
    full_width = rows_whole.shape[1]
    quarter = tokens.shape[1]
    local_heads = quarter // HEAD_DIM
    x_attn = norm_rows(rows_whole.astype(jnp.float32), attn_gain).astype(jnp.bfloat16)
    qkv = jnp.dot(
        x_attn, w_qkv.reshape(full_width, 3 * quarter), preferred_element_type=jnp.float32
    )
    qkv = qkv.astype(jnp.bfloat16).reshape(row_count, 3, quarter)
    suffix_kv = jnp.stack([qkv[:, 1], qkv[:, 2]], axis=1)
    own_slot = prefix_cache[0]
    block_lengths = lengths[0]
    block_groups = groups[0]
    starts = jnp.cumsum(block_lengths) - block_lengths
    req_total = lax.axis_size("req")
    pieces = own_slot.reshape(req_total, PREFIX // req_total, 2, quarter)
    pieces = lax.all_to_all(pieces, "req", split_axis=0, concat_axis=0, tiled=True)
    owned = jnp.take(pieces, owners, axis=0)
    cached = lax.all_gather(owned, "req", axis=1, tiled=True)
    cached = jnp.transpose(cached, (0, 2, 1, 3))
    context = attention(
        qkv[:, 0], qkv[:, 1], qkv[:, 2], cached, block_groups, starts, block_lengths
    )
    context_full = lax.all_gather(context, "exp", axis=1, tiled=True)
    exp_total = lax.axis_size("exp")
    w_out_full = lax.all_to_all(
        jnp.broadcast_to(w_out[None], (exp_total,) + w_out.shape),
        "exp",
        split_axis=0,
        concat_axis=0,
        tiled=True,
    ).reshape(exp_total * w_out.shape[0], w_out.shape[1])
    attn_full = jnp.dot(context_full, w_out_full, preferred_element_type=jnp.float32)
    resid_full = rows_whole.astype(jnp.float32) + attn_full
    x_source = norm_rows(resid_full, moe_gain).astype(jnp.bfloat16)
    column_start = lax.axis_index("exp") * quarter
    resid = lax.dynamic_slice_in_dim(resid_full, column_start, quarter, 1)
    logits = jnp.dot(x_source, w_router, preferred_element_type=jnp.float32)
    gates = jax.nn.sigmoid(jnp.take_along_axis(logits, expert_ids, axis=1)).reshape(-1)
    flat_ids, ranks = slot_ranks(expert_ids, EXPERTS)
    kept, table = slot_table(flat_ids, ranks, CAP, EXPERTS, row_count, TOP)
    columns = x_source.shape[1]
    padded = jnp.concatenate([x_source, jnp.zeros((1, columns), x_source.dtype)], axis=0)
    picked = padded[table].reshape(EXPERTS, 1, CAP, columns)
    local_rows = EXPERTS * SPLIT // req_total
    outgoing_rows = jnp.broadcast_to(picked, (EXPERTS, SPLIT, CAP, columns)).reshape(
        req_total, local_rows, CAP, columns
    )
    partial_out = expert_apply(
        lax.all_to_all(outgoing_rows, "req", split_axis=0, concat_axis=0, tiled=True), w_in, w_down
    )
    returned = lax.all_to_all(
        partial_out.astype(jnp.bfloat16), "req", split_axis=0, concat_axis=0, tiled=True
    ).astype(partial_out.dtype)
    block_count, _, _, out_columns = returned.shape
    pair_column = flat_ids * (SPLIT * CAP) + jnp.minimum(ranks, CAP - 1)
    pair_scale = jnp.where(kept, gates, 0.0)
    columns_all = lax.broadcasted_iota(jnp.int32, (row_count * TOP, block_count * CAP), 1)
    offset = columns_all - pair_column[:, None]
    hit = (offset == 0) | (offset == CAP)
    selection = jnp.where(hit, pair_scale[:, None], 0.0).reshape(row_count, TOP, -1).sum(axis=1)
    mixture = jnp.dot(
        selection,
        returned.reshape(block_count * CAP, out_columns).astype(jnp.float32),
        precision=lax.Precision.HIGHEST,
        preferred_element_type=jnp.float32,
    )
    blocks = jnp.transpose(
        mixture.astype(jnp.bfloat16).reshape(row_count, exp_total, quarter), (1, 0, 2)
    )
    moe_part = jnp.sum(
        lax.all_to_all(blocks, "exp", split_axis=0, concat_axis=0, tiled=True).astype(
            jnp.float32
        ),
        axis=0,
    )
    hidden_out = (resid + moe_part).astype(jnp.bfloat16)
    return (hidden_out, suffix_kv)


def solution(mesh):
    return jax.shard_map(
        shards,
        mesh=mesh,
        in_specs=(
            P("req", "exp"),
            P("req", None),
            P("req", None),
            P(),
            P("req", None, None, "exp"),
            P(),
            P(None, None, "exp"),
            P("exp", None),
            P(),
            P(),
            P("req", None),
            P("req", None, None, "exp"),
            P("req", "exp", None),
        ),
        out_specs=(P("req", "exp"), P("req", None, "exp")),
        check_vma=False,
    )
```

```python
import math

import jax
import jax.numpy as jnp
from jax import lax
from jax.sharding import PartitionSpec as P
from jax.experimental import pallas as pl
from jax.experimental.pallas import tpu as pltpu

HEAD_DIM = 64
EXPERTS = 16
TOP = 2
SPLIT = 2
GROUPS = 4
PREFIX = 2048
REQ_DEV = 4
SUF_MOST = 128
CAP = 40
WINDOW = SUF_MOST + 16


epsilon = 1e-06


def spread(shard, axis, root):
    mine = lax.axis_index(axis) == root
    return lax.psum(jnp.where(mine, shard, jnp.zeros_like(shard)), axis)


def norm_rows(values, gain):
    squares = jnp.sum(values * values, axis=1)
    return values * lax.rsqrt(squares / values.shape[1] + epsilon)[:, None] * gain


def request_context(query_all, key_all, value_all, prefix_kv, start, length, window):
    row_count = query_all.shape[0]
    first = jnp.minimum(start, row_count - window)
    query_win = lax.dynamic_slice_in_dim(query_all, first, window, 0)
    key_win = lax.dynamic_slice_in_dim(key_all, first, window, 0)
    value_win = lax.dynamic_slice_in_dim(value_all, first, window, 0)
    keys = jnp.concatenate([prefix_kv[:, 0], key_win], axis=0)
    values = jnp.concatenate([prefix_kv[:, 1], value_win], axis=0)
    scores = jnp.einsum(
        "qhd,khd->hqk", query_win, keys, preferred_element_type=jnp.float32
    ) / math.sqrt(query_all.shape[2])
    positions = first + jnp.arange(window, dtype=jnp.int32)
    suffix_ok = (positions[None, :] <= positions[:, None]) & (positions[None, :] >= start)
    allowed = jnp.concatenate([jnp.ones((window, prefix_kv.shape[0]), bool), suffix_ok], axis=1)
    scores = jnp.where(allowed[None], scores, -1e30)
    highest = jnp.max(scores, axis=-1, keepdims=True)
    weight = jnp.exp(scores - highest)
    totals = jnp.sum(weight, axis=-1)
    context = jnp.einsum(
        "hqk,khd->qhd", weight.astype(jnp.bfloat16), values, preferred_element_type=jnp.float32
    )
    context = context / jnp.transpose(totals)[:, :, None]
    inside = (positions >= start) & (positions < start + length)
    context = context * inside[:, None, None].astype(jnp.float32)
    placed = jnp.zeros((row_count,) + context.shape[1:], jnp.float32)
    return lax.dynamic_update_slice_in_dim(placed, context, first, 0)


def attention_kernel(
    group_ref, start_ref, length_ref, query_ref, key_ref, value_ref, prefix_ref, out_ref
):
    request = pl.program_id(0)

    @pl.when(request == 0)
    def _():
        out_ref[...] = jnp.zeros_like(out_ref)

    start = start_ref[request]
    stop = start + length_ref[request]
    total_rows, width = query_ref.shape
    rows = WINDOW
    first = pl.multiple_of(jnp.minimum((start // 16) * 16, total_rows - rows), 16)
    row_ids = first + lax.broadcasted_iota(jnp.int32, (rows, rows), 0)
    col_ids = first + lax.broadcasted_iota(jnp.int32, (rows, rows), 1)
    suffix_ok = (col_ids <= row_ids) & (col_ids >= start)
    lane_head = lax.broadcasted_iota(jnp.int32, (1, width), 1) // HEAD_DIM
    query = query_ref[pl.ds(first, rows), :]
    keys = key_ref[pl.ds(first, rows), :]
    values = value_ref[pl.ds(first, rows), :]
    prefix_keys = prefix_ref[0, 0]
    prefix_values = prefix_ref[0, 1]
    scale = 1.0 / math.sqrt(HEAD_DIM)
    contract = (((1,), (1,)), ((), ()))
    context = jnp.zeros((rows, width), jnp.float32)
    for head in range(width // HEAD_DIM):
        in_head = lane_head == head
        query_h = jnp.where(in_head, query, jnp.zeros_like(query))
        score_pre = lax.dot_general(
            query_h, prefix_keys, contract, preferred_element_type=jnp.float32
        ) * scale
        score_suf = lax.dot_general(
            query_h, keys, contract, preferred_element_type=jnp.float32
        ) * scale
        score_suf = jnp.where(suffix_ok, score_suf, -1e30)
        highest = jnp.maximum(
            jnp.max(score_pre, axis=1, keepdims=True), jnp.max(score_suf, axis=1, keepdims=True)
        )
        weight_pre = jnp.exp(score_pre - highest)
        weight_suf = jnp.exp(score_suf - highest)
        totals = jnp.sum(weight_pre, axis=1, keepdims=True) + jnp.sum(
            weight_suf, axis=1, keepdims=True
        )
        mixed = jnp.dot(
            weight_pre.astype(jnp.bfloat16), prefix_values, preferred_element_type=jnp.float32
        ) + jnp.dot(weight_suf.astype(jnp.bfloat16), values, preferred_element_type=jnp.float32)
        context = context + jnp.where(in_head, mixed / totals, 0.0)
    row_in = first + lax.broadcasted_iota(jnp.int32, (rows, 1), 0)
    inside = (row_in >= start) & (row_in < stop)
    out_ref[pl.ds(first, rows), :] = jnp.where(
        inside, context.astype(out_ref.dtype), out_ref[pl.ds(first, rows), :]
    )


def attention(query, keys, values, prefix, block_groups, starts, block_lengths, interpret=False):
    rows, width = query.shape
    slots = prefix.shape[0]
    full = lambda i, g, s, n: (0, 0)
    grid_spec = pltpu.PrefetchScalarGridSpec(
        num_scalar_prefetch=3,
        grid=(block_groups.shape[0],),
        in_specs=[
            pl.BlockSpec((rows, width), full),
            pl.BlockSpec((rows, width), full),
            pl.BlockSpec((rows, width), full),
            pl.BlockSpec((1, 2, PREFIX, width), lambda i, g, s, n: (g[i], 0, 0, 0)),
        ],
        out_specs=pl.BlockSpec((rows, width), full),
    )
    flops = 4 * 2 * 2 * WINDOW * (PREFIX + WINDOW) * width * block_groups.shape[0]
    return pl.pallas_call(
        attention_kernel,
        grid_spec=grid_spec,
        out_shape=jax.ShapeDtypeStruct((rows, width), jnp.bfloat16),
        compiler_params=pltpu.CompilerParams(dimension_semantics=("arbitrary",)),
        interpret=interpret,
        cost_estimate=pl.CostEstimate(
            flops=flops,
            transcendentals=4 * WINDOW * (PREFIX + WINDOW) * block_groups.shape[0],
            bytes_accessed=slots * 2 * PREFIX * width * 2 + 4 * rows * width * 2,
        ),
    )(
        jnp.clip(block_groups, 0, slots - 1),
        starts,
        block_lengths,
        query,
        keys,
        values,
        prefix,
    )


def slot_ranks(identity, experts):
    flat_ids = identity.reshape(-1)
    hits = (flat_ids[:, None] == jnp.arange(experts, dtype=jnp.int32)[None, :]).astype(jnp.int32)
    before = jnp.cumsum(hits, axis=0) - hits
    return (flat_ids, jnp.sum(before * hits, axis=1))


def slot_table(flat_ids, ranks, capacity, experts, row_count, topk):
    kept = ranks < capacity
    target = jnp.where(kept, flat_ids * capacity + ranks, experts * capacity)
    source = jnp.arange(flat_ids.shape[0], dtype=jnp.int32) // topk
    table = (
        jnp.full((experts * capacity,), row_count, jnp.int32).at[target].set(source, mode="drop")
    )
    return (kept, table)


def expert_apply(slots, weight_in, weight_down):
    joined = jnp.einsum("slcd,ldgh->slcgh", slots, weight_in, preferred_element_type=jnp.float32)
    units = (jax.nn.gelu(joined[:, :, :, 0], approximate=True) * joined[:, :, :, 1]).astype(
        jnp.bfloat16
    )
    return jnp.einsum("slch,lhd->slcd", units, weight_down, preferred_element_type=jnp.float32)


def shards(
    tokens,
    lengths,
    groups,
    owners,
    prefix_cache,
    attn_gain,
    w_qkv,
    w_out,
    moe_gain,
    w_router,
    expert_ids,
    w_in,
    w_down,
):
    rows_whole = lax.all_gather(tokens, "exp", axis=1, tiled=True)
    row_count = rows_whole.shape[0]
    full_width = rows_whole.shape[1]
    quarter = tokens.shape[1]
    local_heads = quarter // HEAD_DIM
    x_attn = norm_rows(rows_whole.astype(jnp.float32), attn_gain).astype(jnp.bfloat16)
    qkv = jnp.dot(
        x_attn, w_qkv.reshape(full_width, 3 * quarter), preferred_element_type=jnp.float32
    )
    qkv = qkv.astype(jnp.bfloat16).reshape(row_count, 3, quarter)
    suffix_kv = jnp.stack([qkv[:, 1], qkv[:, 2]], axis=1)
    own_slot = prefix_cache[0]
    block_lengths = lengths[0]
    block_groups = groups[0]
    starts = jnp.cumsum(block_lengths) - block_lengths
    req_total = lax.axis_size("req")
    pieces = own_slot.reshape(req_total, PREFIX // req_total, 2, quarter)
    pieces = lax.all_to_all(pieces, "req", split_axis=0, concat_axis=0, tiled=True)
    owned = jnp.take(pieces, owners, axis=0)
    cached = lax.all_gather(owned, "req", axis=1, tiled=True)
    cached = jnp.transpose(cached, (0, 2, 1, 3))
    context = attention(
        qkv[:, 0], qkv[:, 1], qkv[:, 2], cached, block_groups, starts, block_lengths
    )
    context_full = lax.all_gather(context, "exp", axis=1, tiled=True)
    exp_total = lax.axis_size("exp")
    w_out_full = lax.all_to_all(
        jnp.broadcast_to(w_out[None], (exp_total,) + w_out.shape),
        "exp",
        split_axis=0,
        concat_axis=0,
        tiled=True,
    ).reshape(exp_total * w_out.shape[0], w_out.shape[1])
    attn_full = jnp.dot(context_full, w_out_full, preferred_element_type=jnp.float32)
    resid_full = rows_whole.astype(jnp.float32) + attn_full
    x_source = norm_rows(resid_full, moe_gain).astype(jnp.bfloat16)
    column_start = lax.axis_index("exp") * quarter
    resid = lax.dynamic_slice_in_dim(resid_full, column_start, quarter, 1)
    logits = jnp.dot(x_source, w_router, preferred_element_type=jnp.float32)
    gates = jax.nn.sigmoid(jnp.take_along_axis(logits, expert_ids, axis=1)).reshape(-1)
    flat_ids, ranks = slot_ranks(expert_ids, EXPERTS)
    kept, table = slot_table(flat_ids, ranks, CAP, EXPERTS, row_count, TOP)
    columns = x_source.shape[1]
    padded = jnp.concatenate([x_source, jnp.zeros((1, columns), x_source.dtype)], axis=0)
    picked = padded[table].reshape(EXPERTS, 1, CAP, columns)
    local_rows = EXPERTS * SPLIT // req_total
    outgoing_rows = jnp.broadcast_to(picked, (EXPERTS, SPLIT, CAP, columns)).reshape(
        req_total, local_rows, CAP, columns
    )
    partial_out = expert_apply(
        lax.all_to_all(outgoing_rows, "req", split_axis=0, concat_axis=0, tiled=True), w_in, w_down
    )
    returned = lax.all_to_all(
        partial_out.astype(jnp.bfloat16), "req", split_axis=0, concat_axis=0, tiled=True
    ).astype(partial_out.dtype)
    block_count, _, _, out_columns = returned.shape
    pair_column = flat_ids * (SPLIT * CAP) + jnp.minimum(ranks, CAP - 1)
    pair_scale = jnp.where(kept, gates, 0.0)
    columns_all = lax.broadcasted_iota(jnp.int32, (row_count * TOP, block_count * CAP), 1)
    offset = columns_all - pair_column[:, None]
    hit = (offset == 0) | (offset == CAP)
    selection = jnp.where(hit, pair_scale[:, None], 0.0).reshape(row_count, TOP, -1).sum(axis=1)
    mixture = jnp.dot(
        selection,
        returned.reshape(block_count * CAP, out_columns).astype(jnp.float32),
        precision=lax.Precision.HIGHEST,
        preferred_element_type=jnp.float32,
    )
    blocks = jnp.transpose(
        mixture.astype(jnp.bfloat16).reshape(row_count, exp_total, quarter), (1, 0, 2)
    )
    moe_part = jnp.sum(
        lax.all_to_all(blocks, "exp", split_axis=0, concat_axis=0, tiled=True).astype(
            jnp.float32
        ),
        axis=0,
    )
    hidden_out = (resid + moe_part).astype(jnp.bfloat16)
    return (hidden_out, suffix_kv)


def solution(mesh):
    return jax.shard_map(
        shards,
        mesh=mesh,
        in_specs=(
            P("req", "exp"),
            P("req", None),
            P("req", None),
            P(),
            P("req", None, None, "exp"),
            P(),
            P(None, None, "exp"),
            P("exp", None),
            P(),
            P(),
            P("req", None),
            P("req", None, None, "exp"),
            P("req", "exp", None),
        ),
        out_specs=(P("req", "exp"), P("req", None, "exp")),
        check_vma=False,
    )
```

```python
import math

import jax
import jax.numpy as jnp
from jax import lax
from jax.sharding import PartitionSpec as P
from jax.experimental import pallas as pl
from jax.experimental.pallas import tpu as pltpu

HEAD_DIM = 64
EXPERTS = 16
TOP = 2
SPLIT = 2
GROUPS = 4
PREFIX = 2048
REQ_DEV = 4
SUF_MOST = 128
CAP = 40
WINDOW = SUF_MOST + 16


epsilon = 1e-06


def spread(shard, axis, root):
    mine = lax.axis_index(axis) == root
    return lax.psum(jnp.where(mine, shard, jnp.zeros_like(shard)), axis)


def norm_rows(values, gain):
    squares = jnp.sum(values * values, axis=1)
    return values * lax.rsqrt(squares / values.shape[1] + epsilon)[:, None] * gain


def request_context(query_all, key_all, value_all, prefix_kv, start, length, window):
    row_count = query_all.shape[0]
    first = jnp.minimum(start, row_count - window)
    query_win = lax.dynamic_slice_in_dim(query_all, first, window, 0)
    key_win = lax.dynamic_slice_in_dim(key_all, first, window, 0)
    value_win = lax.dynamic_slice_in_dim(value_all, first, window, 0)
    keys = jnp.concatenate([prefix_kv[:, 0], key_win], axis=0)
    values = jnp.concatenate([prefix_kv[:, 1], value_win], axis=0)
    scores = jnp.einsum(
        "qhd,khd->hqk", query_win, keys, preferred_element_type=jnp.float32
    ) / math.sqrt(query_all.shape[2])
    positions = first + jnp.arange(window, dtype=jnp.int32)
    suffix_ok = (positions[None, :] <= positions[:, None]) & (positions[None, :] >= start)
    allowed = jnp.concatenate([jnp.ones((window, prefix_kv.shape[0]), bool), suffix_ok], axis=1)
    scores = jnp.where(allowed[None], scores, -1e30)
    highest = jnp.max(scores, axis=-1, keepdims=True)
    weight = jnp.exp(scores - highest)
    totals = jnp.sum(weight, axis=-1)
    context = jnp.einsum(
        "hqk,khd->qhd", weight.astype(jnp.bfloat16), values, preferred_element_type=jnp.float32
    )
    context = context / jnp.transpose(totals)[:, :, None]
    inside = (positions >= start) & (positions < start + length)
    context = context * inside[:, None, None].astype(jnp.float32)
    placed = jnp.zeros((row_count,) + context.shape[1:], jnp.float32)
    return lax.dynamic_update_slice_in_dim(placed, context, first, 0)


def attention_kernel(
    group_ref, start_ref, length_ref, query_ref, key_ref, value_ref, prefix_ref, last_ref, out_ref
):
    request = pl.program_id(0)

    @pl.when(request == 0)
    def _():
        out_ref[...] = jnp.zeros_like(out_ref)

    start = start_ref[request]
    stop = start + length_ref[request]
    total_rows, width = query_ref.shape
    rows = WINDOW
    first = pl.multiple_of(jnp.minimum((start // 16) * 16, total_rows - rows), 16)
    row_ids = first + lax.broadcasted_iota(jnp.int32, (rows, rows), 0)
    col_ids = first + lax.broadcasted_iota(jnp.int32, (rows, rows), 1)
    suffix_ok = (col_ids <= row_ids) & (col_ids >= start)
    lane_head = lax.broadcasted_iota(jnp.int32, (1, width), 1) // HEAD_DIM
    query = query_ref[pl.ds(first, rows), :]
    keys = key_ref[pl.ds(first, rows), :]
    values = value_ref[pl.ds(first, rows), :]
    is_last = group_ref[request] == GROUPS - 1
    prefix_keys = jnp.where(is_last, last_ref[0, 0], prefix_ref[0, 0])
    prefix_values = jnp.where(is_last, last_ref[0, 1], prefix_ref[0, 1])
    scale = 1.0 / math.sqrt(HEAD_DIM)
    contract = (((1,), (1,)), ((), ()))
    context = jnp.zeros((rows, width), jnp.float32)
    for head in range(width // HEAD_DIM):
        in_head = lane_head == head
        query_h = jnp.where(in_head, query, jnp.zeros_like(query))
        score_pre = lax.dot_general(
            query_h, prefix_keys, contract, preferred_element_type=jnp.float32
        ) * scale
        score_suf = lax.dot_general(
            query_h, keys, contract, preferred_element_type=jnp.float32
        ) * scale
        score_suf = jnp.where(suffix_ok, score_suf, -1e30)
        highest = jnp.maximum(
            jnp.max(score_pre, axis=1, keepdims=True), jnp.max(score_suf, axis=1, keepdims=True)
        )
        weight_pre = jnp.exp(score_pre - highest)
        weight_suf = jnp.exp(score_suf - highest)
        totals = jnp.sum(weight_pre, axis=1, keepdims=True) + jnp.sum(
            weight_suf, axis=1, keepdims=True
        )
        mixed = jnp.dot(
            weight_pre.astype(jnp.bfloat16), prefix_values, preferred_element_type=jnp.float32
        ) + jnp.dot(weight_suf.astype(jnp.bfloat16), values, preferred_element_type=jnp.float32)
        context = context + jnp.where(in_head, mixed / totals, 0.0)
    row_in = first + lax.broadcasted_iota(jnp.int32, (rows, 1), 0)
    inside = (row_in >= start) & (row_in < stop)
    out_ref[pl.ds(first, rows), :] = jnp.where(
        inside, context.astype(out_ref.dtype), out_ref[pl.ds(first, rows), :]
    )


def attention(query, keys, values, prefix, block_groups, starts, block_lengths, interpret=False):
    rows, width = query.shape
    prefix, last = prefix
    slots = prefix.shape[0]
    full = lambda i, g, s, n: (0, 0)
    grid_spec = pltpu.PrefetchScalarGridSpec(
        num_scalar_prefetch=3,
        grid=(block_groups.shape[0],),
        in_specs=[
            pl.BlockSpec((rows, width), full),
            pl.BlockSpec((rows, width), full),
            pl.BlockSpec((rows, width), full),
            pl.BlockSpec(
                (1, 2, PREFIX, width), lambda i, g, s, n: (jnp.minimum(g[i], GROUPS - 2), 0, 0, 0)
            ),
            pl.BlockSpec((1, 2, PREFIX, width), lambda i, g, s, n: (0, 0, 0, 0)),
        ],
        out_specs=pl.BlockSpec((rows, width), full),
    )
    flops = 4 * 2 * 2 * WINDOW * (PREFIX + WINDOW) * width * block_groups.shape[0]
    return pl.pallas_call(
        attention_kernel,
        grid_spec=grid_spec,
        out_shape=jax.ShapeDtypeStruct((rows, width), jnp.bfloat16),
        compiler_params=pltpu.CompilerParams(dimension_semantics=("arbitrary",)),
        interpret=interpret,
        cost_estimate=pl.CostEstimate(
            flops=flops,
            transcendentals=4 * WINDOW * (PREFIX + WINDOW) * block_groups.shape[0],
            bytes_accessed=slots * 2 * PREFIX * width * 2 + 4 * rows * width * 2,
        ),
    )(
        jnp.clip(block_groups, 0, GROUPS - 1),
        starts,
        block_lengths,
        query,
        keys,
        values,
        prefix,
        last,
    )


def slot_ranks(identity, experts):
    flat_ids = identity.reshape(-1)
    hits = (flat_ids[:, None] == jnp.arange(experts, dtype=jnp.int32)[None, :]).astype(jnp.int32)
    before = jnp.cumsum(hits, axis=0) - hits
    return (flat_ids, jnp.sum(before * hits, axis=1))


def slot_table(flat_ids, ranks, capacity, experts, row_count, topk):
    kept = ranks < capacity
    target = jnp.where(kept, flat_ids * capacity + ranks, experts * capacity)
    source = jnp.arange(flat_ids.shape[0], dtype=jnp.int32) // topk
    table = (
        jnp.full((experts * capacity,), row_count, jnp.int32).at[target].set(source, mode="drop")
    )
    return (kept, table)


def expert_apply(slots, weight_in, weight_down):
    joined = jnp.einsum("slcd,ldgh->slcgh", slots, weight_in, preferred_element_type=jnp.float32)
    units = (jax.nn.gelu(joined[:, :, :, 0], approximate=True) * joined[:, :, :, 1]).astype(
        jnp.bfloat16
    )
    return jnp.einsum("slch,lhd->slcd", units, weight_down, preferred_element_type=jnp.float32)


def shards(
    tokens,
    lengths,
    groups,
    owners,
    prefix_cache,
    attn_gain,
    w_qkv,
    w_out,
    moe_gain,
    w_router,
    expert_ids,
    w_in,
    w_down,
):
    rows_whole = lax.all_gather(tokens, "exp", axis=1, tiled=True)
    row_count = rows_whole.shape[0]
    full_width = rows_whole.shape[1]
    quarter = tokens.shape[1]
    local_heads = quarter // HEAD_DIM
    x_attn = norm_rows(rows_whole.astype(jnp.float32), attn_gain).astype(jnp.bfloat16)
    qkv = jnp.dot(
        x_attn, w_qkv.reshape(full_width, 3 * quarter), preferred_element_type=jnp.float32
    )
    qkv = qkv.astype(jnp.bfloat16).reshape(row_count, 3, quarter)
    suffix_kv = jnp.stack([qkv[:, 1], qkv[:, 2]], axis=1)
    own_slot = prefix_cache[0]
    block_lengths = lengths[0]
    block_groups = groups[0]
    starts = jnp.cumsum(block_lengths) - block_lengths
    req_total = lax.axis_size("req")
    pieces = own_slot.reshape(req_total, PREFIX // req_total, 2, quarter)
    pieces = lax.all_to_all(pieces, "req", split_axis=0, concat_axis=0, tiled=True)
    owned = jnp.take(pieces, owners, axis=0)
    cached = lax.all_gather(owned[: GROUPS - 1], "req", axis=1, tiled=True)
    cached = jnp.transpose(cached, (0, 2, 1, 3))
    last_piece = jnp.transpose(owned[GROUPS - 1], (1, 0, 2))
    last = lax.all_to_all(
        jnp.broadcast_to(last_piece[None], (req_total,) + last_piece.shape),
        "req",
        split_axis=0,
        concat_axis=0,
        tiled=True,
    )
    last = jnp.transpose(last, (1, 0, 2, 3)).reshape(1, 2, PREFIX, quarter)
    context = attention(
        qkv[:, 0], qkv[:, 1], qkv[:, 2], (cached, last), block_groups, starts, block_lengths
    )
    context_full = lax.all_gather(context, "exp", axis=1, tiled=True)
    exp_total = lax.axis_size("exp")
    w_out_full = lax.all_to_all(
        jnp.broadcast_to(w_out[None], (exp_total,) + w_out.shape),
        "exp",
        split_axis=0,
        concat_axis=0,
        tiled=True,
    ).reshape(exp_total * w_out.shape[0], w_out.shape[1])
    attn_full = jnp.dot(context_full, w_out_full, preferred_element_type=jnp.float32)
    resid_full = rows_whole.astype(jnp.float32) + attn_full
    x_source = norm_rows(resid_full, moe_gain).astype(jnp.bfloat16)
    column_start = lax.axis_index("exp") * quarter
    resid = lax.dynamic_slice_in_dim(resid_full, column_start, quarter, 1)
    logits = jnp.dot(x_source, w_router, preferred_element_type=jnp.float32)
    gates = jax.nn.sigmoid(jnp.take_along_axis(logits, expert_ids, axis=1)).reshape(-1)
    flat_ids, ranks = slot_ranks(expert_ids, EXPERTS)
    kept, table = slot_table(flat_ids, ranks, CAP, EXPERTS, row_count, TOP)
    columns = x_source.shape[1]
    padded = jnp.concatenate([x_source, jnp.zeros((1, columns), x_source.dtype)], axis=0)
    picked = padded[table].reshape(EXPERTS, 1, CAP, columns)
    local_rows = EXPERTS * SPLIT // req_total
    outgoing_rows = jnp.broadcast_to(picked, (EXPERTS, SPLIT, CAP, columns)).reshape(
        req_total, local_rows, CAP, columns
    )
    partial_out = expert_apply(
        lax.all_to_all(outgoing_rows, "req", split_axis=0, concat_axis=0, tiled=True), w_in, w_down
    )
    returned = lax.all_to_all(
        partial_out.astype(jnp.bfloat16), "req", split_axis=0, concat_axis=0, tiled=True
    ).astype(partial_out.dtype)
    block_count, _, _, out_columns = returned.shape
    pair_column = flat_ids * (SPLIT * CAP) + jnp.minimum(ranks, CAP - 1)
    pair_scale = jnp.where(kept, gates, 0.0)
    columns_all = lax.broadcasted_iota(jnp.int32, (row_count * TOP, block_count * CAP), 1)
    offset = columns_all - pair_column[:, None]
    hit = (offset == 0) | (offset == CAP)
    selection = jnp.where(hit, pair_scale[:, None], 0.0).reshape(row_count, TOP, -1).sum(axis=1)
    mixture = jnp.dot(
        selection,
        returned.reshape(block_count * CAP, out_columns).astype(jnp.float32),
        precision=lax.Precision.HIGHEST,
        preferred_element_type=jnp.float32,
    )
    blocks = jnp.transpose(
        mixture.astype(jnp.bfloat16).reshape(row_count, exp_total, quarter), (1, 0, 2)
    )
    moe_part = jnp.sum(
        lax.all_to_all(blocks, "exp", split_axis=0, concat_axis=0, tiled=True).astype(
            jnp.float32
        ),
        axis=0,
    )
    hidden_out = (resid + moe_part).astype(jnp.bfloat16)
    return (hidden_out, suffix_kv)


def solution(mesh):
    return jax.shard_map(
        shards,
        mesh=mesh,
        in_specs=(
            P("req", "exp"),
            P("req", None),
            P("req", None),
            P(),
            P("req", None, None, "exp"),
            P(),
            P(None, None, "exp"),
            P("exp", None),
            P(),
            P(),
            P("req", None),
            P("req", None, None, "exp"),
            P("req", "exp", None),
        ),
        out_specs=(P("req", "exp"), P("req", None, "exp")),
        check_vma=False,
    )
```

```python
import math

import jax
import jax.numpy as jnp
from jax import lax
from jax.sharding import PartitionSpec as P
from jax.experimental import pallas as pl
from jax.experimental.pallas import tpu as pltpu

HEAD_DIM = 64
EXPERTS = 16
TOP = 2
SPLIT = 2
GROUPS = 4
PREFIX = 2048
REQ_DEV = 4
SUF_MOST = 128
CAP = 40
WINDOW = SUF_MOST + 16


epsilon = 1e-06


def spread(shard, axis, root):
    mine = lax.axis_index(axis) == root
    return lax.psum(jnp.where(mine, shard, jnp.zeros_like(shard)), axis)


def norm_rows(values, gain):
    squares = jnp.sum(values * values, axis=1)
    return values * lax.rsqrt(squares / values.shape[1] + epsilon)[:, None] * gain


def request_context(query_all, key_all, value_all, prefix_kv, start, length, window):
    row_count = query_all.shape[0]
    first = jnp.minimum(start, row_count - window)
    query_win = lax.dynamic_slice_in_dim(query_all, first, window, 0)
    key_win = lax.dynamic_slice_in_dim(key_all, first, window, 0)
    value_win = lax.dynamic_slice_in_dim(value_all, first, window, 0)
    keys = jnp.concatenate([prefix_kv[:, 0], key_win], axis=0)
    values = jnp.concatenate([prefix_kv[:, 1], value_win], axis=0)
    scores = jnp.einsum(
        "qhd,khd->hqk", query_win, keys, preferred_element_type=jnp.float32
    ) / math.sqrt(query_all.shape[2])
    positions = first + jnp.arange(window, dtype=jnp.int32)
    suffix_ok = (positions[None, :] <= positions[:, None]) & (positions[None, :] >= start)
    allowed = jnp.concatenate([jnp.ones((window, prefix_kv.shape[0]), bool), suffix_ok], axis=1)
    scores = jnp.where(allowed[None], scores, -1e30)
    highest = jnp.max(scores, axis=-1, keepdims=True)
    weight = jnp.exp(scores - highest)
    totals = jnp.sum(weight, axis=-1)
    context = jnp.einsum(
        "hqk,khd->qhd", weight.astype(jnp.bfloat16), values, preferred_element_type=jnp.float32
    )
    context = context / jnp.transpose(totals)[:, :, None]
    inside = (positions >= start) & (positions < start + length)
    context = context * inside[:, None, None].astype(jnp.float32)
    placed = jnp.zeros((row_count,) + context.shape[1:], jnp.float32)
    return lax.dynamic_update_slice_in_dim(placed, context, first, 0)


def attention_kernel(
    group_ref, start_ref, length_ref, query_ref, key_ref, value_ref, prefix_ref, out_ref
):
    request = pl.program_id(0)

    @pl.when(request == 0)
    def _():
        out_ref[...] = jnp.zeros_like(out_ref)

    start = start_ref[request]
    stop = start + length_ref[request]
    total_rows, width = query_ref.shape
    rows = WINDOW
    first = pl.multiple_of(jnp.minimum((start // 16) * 16, total_rows - rows), 16)
    row_ids = first + lax.broadcasted_iota(jnp.int32, (rows, rows), 0)
    col_ids = first + lax.broadcasted_iota(jnp.int32, (rows, rows), 1)
    suffix_ok = (col_ids <= row_ids) & (col_ids >= start)
    lane_head = lax.broadcasted_iota(jnp.int32, (1, width), 1) // HEAD_DIM
    query = query_ref[pl.ds(first, rows), :]
    keys = key_ref[pl.ds(first, rows), :]
    values = value_ref[pl.ds(first, rows), :]
    prefix_keys = prefix_ref[0, 0]
    prefix_values = prefix_ref[0, 1]
    scale = 1.0 / math.sqrt(HEAD_DIM)
    contract = (((1,), (1,)), ((), ()))
    context = jnp.zeros((rows, width), jnp.float32)
    for head in range(width // HEAD_DIM):
        in_head = lane_head == head
        query_h = jnp.where(in_head, query, jnp.zeros_like(query))
        score_pre = lax.dot_general(
            query_h, prefix_keys, contract, preferred_element_type=jnp.float32
        ) * scale
        score_suf = lax.dot_general(
            query_h, keys, contract, preferred_element_type=jnp.float32
        ) * scale
        score_suf = jnp.where(suffix_ok, score_suf, -1e30)
        highest = jnp.maximum(
            jnp.max(score_pre, axis=1, keepdims=True), jnp.max(score_suf, axis=1, keepdims=True)
        )
        weight_pre = jnp.exp(score_pre - highest)
        weight_suf = jnp.exp(score_suf - highest)
        totals = jnp.sum(weight_pre, axis=1, keepdims=True) + jnp.sum(
            weight_suf, axis=1, keepdims=True
        )
        mixed = jnp.dot(
            weight_pre.astype(jnp.bfloat16), prefix_values, preferred_element_type=jnp.float32
        ) + jnp.dot(weight_suf.astype(jnp.bfloat16), values, preferred_element_type=jnp.float32)
        context = context + jnp.where(in_head, mixed / totals, 0.0)
    row_in = first + lax.broadcasted_iota(jnp.int32, (rows, 1), 0)
    inside = (row_in >= start) & (row_in < stop)
    out_ref[pl.ds(first, rows), :] = jnp.where(
        inside, context.astype(out_ref.dtype), out_ref[pl.ds(first, rows), :]
    )


def attention(query, keys, values, prefix, block_groups, starts, block_lengths, interpret=False):
    rows, width = query.shape
    slots = prefix.shape[0]
    full = lambda i, g, s, n: (0, 0)
    grid_spec = pltpu.PrefetchScalarGridSpec(
        num_scalar_prefetch=3,
        grid=(block_groups.shape[0],),
        in_specs=[
            pl.BlockSpec((rows, width), full),
            pl.BlockSpec((rows, width), full),
            pl.BlockSpec((rows, width), full),
            pl.BlockSpec((1, 2, PREFIX, width), lambda i, g, s, n: (g[i], 0, 0, 0)),
        ],
        out_specs=pl.BlockSpec((rows, width), full),
    )
    flops = 4 * 2 * 2 * WINDOW * (PREFIX + WINDOW) * width * block_groups.shape[0]
    return pl.pallas_call(
        attention_kernel,
        grid_spec=grid_spec,
        out_shape=jax.ShapeDtypeStruct((rows, width), jnp.bfloat16),
        compiler_params=pltpu.CompilerParams(dimension_semantics=("arbitrary",)),
        interpret=interpret,
        cost_estimate=pl.CostEstimate(
            flops=flops,
            transcendentals=4 * WINDOW * (PREFIX + WINDOW) * block_groups.shape[0],
            bytes_accessed=slots * 2 * PREFIX * width * 2 + 4 * rows * width * 2,
        ),
    )(
        jnp.clip(block_groups, 0, slots - 1),
        starts,
        block_lengths,
        query,
        keys,
        values,
        prefix,
    )


def slot_ranks(identity, experts):
    flat_ids = identity.reshape(-1)
    hits = (flat_ids[:, None] == jnp.arange(experts, dtype=jnp.int32)[None, :]).astype(jnp.int32)
    before = jnp.cumsum(hits, axis=0) - hits
    return (flat_ids, jnp.sum(before * hits, axis=1))


def slot_table(flat_ids, ranks, capacity, experts, row_count, topk):
    kept = ranks < capacity
    target = jnp.where(kept, flat_ids * capacity + ranks, experts * capacity)
    source = jnp.arange(flat_ids.shape[0], dtype=jnp.int32) // topk
    table = (
        jnp.full((experts * capacity,), row_count, jnp.int32).at[target].set(source, mode="drop")
    )
    return (kept, table)


def expert_apply(slots, weight_in, weight_down):
    joined = jnp.einsum("slcd,ldgh->slcgh", slots, weight_in, preferred_element_type=jnp.float32)
    units = (jax.nn.gelu(joined[:, :, :, 0], approximate=True) * joined[:, :, :, 1]).astype(
        jnp.bfloat16
    )
    return jnp.einsum("slch,lhd->slcd", units, weight_down, preferred_element_type=jnp.float32)


def shards(
    tokens,
    lengths,
    groups,
    owners,
    prefix_cache,
    attn_gain,
    w_qkv,
    w_out,
    moe_gain,
    w_router,
    expert_ids,
    w_in,
    w_down,
):
    rows_whole = lax.all_gather(tokens, "exp", axis=1, tiled=True)
    row_count = rows_whole.shape[0]
    full_width = rows_whole.shape[1]
    quarter = tokens.shape[1]
    local_heads = quarter // HEAD_DIM
    x_attn = norm_rows(rows_whole.astype(jnp.float32), attn_gain).astype(jnp.bfloat16)
    qkv = jnp.dot(
        x_attn, w_qkv.reshape(full_width, 3 * quarter), preferred_element_type=jnp.float32
    )
    qkv = qkv.astype(jnp.bfloat16).reshape(row_count, 3, quarter)
    suffix_kv = jnp.stack([qkv[:, 1], qkv[:, 2]], axis=1)
    own_slot = prefix_cache[0]
    block_lengths = lengths[0]
    block_groups = groups[0]
    starts = jnp.cumsum(block_lengths) - block_lengths
    req_total = lax.axis_size("req")
    pieces = own_slot.reshape(req_total, PREFIX // req_total, 2, quarter)
    pieces = lax.all_to_all(pieces, "req", split_axis=0, concat_axis=0, tiled=True)
    owned = jnp.take(pieces, owners, axis=0)
    cached = lax.all_gather(owned, "req", axis=1, tiled=True)
    cached = jnp.transpose(cached, (0, 2, 1, 3))
    context = attention(
        qkv[:, 0], qkv[:, 1], qkv[:, 2], cached, block_groups, starts, block_lengths
    )
    context_full = lax.all_gather(context, "exp", axis=1, tiled=True)
    exp_total = lax.axis_size("exp")
    w_out_full = lax.all_to_all(
        jnp.broadcast_to(w_out[None], (exp_total,) + w_out.shape),
        "exp",
        split_axis=0,
        concat_axis=0,
        tiled=True,
    ).reshape(exp_total * w_out.shape[0], w_out.shape[1])
    attn_full = jnp.dot(context_full, w_out_full, preferred_element_type=jnp.float32)
    resid_full = rows_whole.astype(jnp.float32) + attn_full
    x_source = norm_rows(resid_full, moe_gain).astype(jnp.bfloat16)
    column_start = lax.axis_index("exp") * quarter
    resid = lax.dynamic_slice_in_dim(resid_full, column_start, quarter, 1)
    logits = jnp.dot(x_source, w_router, preferred_element_type=jnp.float32)
    gates = jax.nn.sigmoid(jnp.take_along_axis(logits, expert_ids, axis=1)).reshape(-1)
    flat_ids, ranks = slot_ranks(expert_ids, EXPERTS)
    kept, table = slot_table(flat_ids, ranks, CAP, EXPERTS, row_count, TOP)
    columns = x_source.shape[1]
    padded = jnp.concatenate([x_source, jnp.zeros((1, columns), x_source.dtype)], axis=0)
    picked = padded[table].reshape(EXPERTS, 1, CAP, columns)
    local_rows = EXPERTS * SPLIT // req_total
    outgoing_rows = jnp.broadcast_to(picked, (EXPERTS, SPLIT, CAP, columns)).reshape(
        req_total, local_rows, CAP, columns
    )
    partial_out = expert_apply(
        lax.all_to_all(outgoing_rows, "req", split_axis=0, concat_axis=0, tiled=True), w_in, w_down
    )
    returned = lax.all_to_all(
        partial_out.astype(jnp.bfloat16), "req", split_axis=0, concat_axis=0, tiled=True
    )
    block_count, _, _, out_columns = returned.shape
    pair_column = flat_ids * (SPLIT * CAP) + jnp.minimum(ranks, CAP - 1)
    pair_scale = jnp.where(kept, gates, 0.0)
    columns_all = lax.broadcasted_iota(jnp.int32, (row_count * TOP, block_count * CAP), 1)
    offset = columns_all - pair_column[:, None]
    hit = (offset == 0) | (offset == CAP)
    selection = jnp.where(hit, pair_scale[:, None], 0.0).reshape(row_count, TOP, -1).sum(axis=1)
    selection_hi = selection.astype(jnp.bfloat16)
    selection_lo = (selection - selection_hi.astype(jnp.float32)).astype(jnp.bfloat16)
    returned_rows = returned.reshape(block_count * CAP, out_columns)
    mixture = jnp.dot(selection_hi, returned_rows, preferred_element_type=jnp.float32) + jnp.dot(
        selection_lo, returned_rows, preferred_element_type=jnp.float32
    )
    blocks = jnp.transpose(
        mixture.astype(jnp.bfloat16).reshape(row_count, exp_total, quarter), (1, 0, 2)
    )
    moe_part = jnp.sum(
        lax.all_to_all(blocks, "exp", split_axis=0, concat_axis=0, tiled=True).astype(
            jnp.float32
        ),
        axis=0,
    )
    hidden_out = (resid + moe_part).astype(jnp.bfloat16)
    return (hidden_out, suffix_kv)


def solution(mesh):
    return jax.shard_map(
        shards,
        mesh=mesh,
        in_specs=(
            P("req", "exp"),
            P("req", None),
            P("req", None),
            P(),
            P("req", None, None, "exp"),
            P(),
            P(None, None, "exp"),
            P("exp", None),
            P(),
            P(),
            P("req", None),
            P("req", None, None, "exp"),
            P("req", "exp", None),
        ),
        out_specs=(P("req", "exp"), P("req", None, "exp")),
        check_vma=False,
    )
```

```python
import math

import jax
import jax.numpy as jnp
from jax import lax
from jax.sharding import PartitionSpec as P
from jax.experimental import pallas as pl
from jax.experimental.pallas import tpu as pltpu

HEAD_DIM = 64
EXPERTS = 16
TOP = 2
SPLIT = 2
GROUPS = 4
PREFIX = 2048
REQ_DEV = 4
SUF_MOST = 128
CAP = 40
WINDOW = SUF_MOST + 16


epsilon = 1e-06


def spread(shard, axis, root):
    mine = lax.axis_index(axis) == root
    return lax.psum(jnp.where(mine, shard, jnp.zeros_like(shard)), axis)


def norm_rows(values, gain):
    squares = jnp.sum(values * values, axis=1)
    return values * lax.rsqrt(squares / values.shape[1] + epsilon)[:, None] * gain


def request_context(query_all, key_all, value_all, prefix_kv, start, length, window):
    row_count = query_all.shape[0]
    first = jnp.minimum(start, row_count - window)
    query_win = lax.dynamic_slice_in_dim(query_all, first, window, 0)
    key_win = lax.dynamic_slice_in_dim(key_all, first, window, 0)
    value_win = lax.dynamic_slice_in_dim(value_all, first, window, 0)
    keys = jnp.concatenate([prefix_kv[:, 0], key_win], axis=0)
    values = jnp.concatenate([prefix_kv[:, 1], value_win], axis=0)
    scores = jnp.einsum(
        "qhd,khd->hqk", query_win, keys, preferred_element_type=jnp.float32
    ) / math.sqrt(query_all.shape[2])
    positions = first + jnp.arange(window, dtype=jnp.int32)
    suffix_ok = (positions[None, :] <= positions[:, None]) & (positions[None, :] >= start)
    allowed = jnp.concatenate([jnp.ones((window, prefix_kv.shape[0]), bool), suffix_ok], axis=1)
    scores = jnp.where(allowed[None], scores, -1e30)
    highest = jnp.max(scores, axis=-1, keepdims=True)
    weight = jnp.exp(scores - highest)
    totals = jnp.sum(weight, axis=-1)
    context = jnp.einsum(
        "hqk,khd->qhd", weight.astype(jnp.bfloat16), values, preferred_element_type=jnp.float32
    )
    context = context / jnp.transpose(totals)[:, :, None]
    inside = (positions >= start) & (positions < start + length)
    context = context * inside[:, None, None].astype(jnp.float32)
    placed = jnp.zeros((row_count,) + context.shape[1:], jnp.float32)
    return lax.dynamic_update_slice_in_dim(placed, context, first, 0)


def attention_kernel(
    group_ref, start_ref, length_ref, query_ref, key_ref, value_ref, prefix_ref, out_ref
):
    request = pl.program_id(0)

    @pl.when(request == 0)
    def _():
        out_ref[...] = jnp.zeros_like(out_ref)

    start = start_ref[request]
    stop = start + length_ref[request]
    total_rows, width = query_ref.shape
    rows = WINDOW
    first = pl.multiple_of(jnp.minimum((start // 16) * 16, total_rows - rows), 16)
    row_ids = first + lax.broadcasted_iota(jnp.int32, (rows, rows), 0)
    col_ids = first + lax.broadcasted_iota(jnp.int32, (rows, rows), 1)
    suffix_ok = (col_ids <= row_ids) & (col_ids >= start)
    lane_head = lax.broadcasted_iota(jnp.int32, (1, width), 1) // HEAD_DIM
    query = query_ref[pl.ds(first, rows), :]
    keys = key_ref[pl.ds(first, rows), :]
    values = value_ref[pl.ds(first, rows), :]
    prefix_keys = prefix_ref[0, 0]
    prefix_values = prefix_ref[0, 1]
    scale = 1.0 / math.sqrt(HEAD_DIM)
    contract = (((1,), (1,)), ((), ()))
    context = jnp.zeros((rows, width), jnp.float32)
    for head in range(width // HEAD_DIM):
        in_head = lane_head == head
        query_h = jnp.where(in_head, query, jnp.zeros_like(query))
        score_pre = lax.dot_general(
            query_h, prefix_keys, contract, preferred_element_type=jnp.float32
        ) * scale
        score_suf = lax.dot_general(
            query_h, keys, contract, preferred_element_type=jnp.float32
        ) * scale
        score_suf = jnp.where(suffix_ok, score_suf, -1e30)
        highest = jnp.maximum(
            jnp.max(score_pre, axis=1, keepdims=True), jnp.max(score_suf, axis=1, keepdims=True)
        )
        weight_pre = jnp.exp(score_pre - highest)
        weight_suf = jnp.exp(score_suf - highest)
        totals = jnp.sum(weight_pre, axis=1, keepdims=True) + jnp.sum(
            weight_suf, axis=1, keepdims=True
        )
        mixed = jnp.dot(
            weight_pre.astype(jnp.bfloat16), prefix_values, preferred_element_type=jnp.float32
        ) + jnp.dot(weight_suf.astype(jnp.bfloat16), values, preferred_element_type=jnp.float32)
        context = context + jnp.where(in_head, mixed / totals, 0.0)
    row_in = first + lax.broadcasted_iota(jnp.int32, (rows, 1), 0)
    inside = (row_in >= start) & (row_in < stop)
    out_ref[pl.ds(first, rows), :] = jnp.where(
        inside, context.astype(out_ref.dtype), out_ref[pl.ds(first, rows), :]
    )


def attention(query, keys, values, prefix, block_groups, starts, block_lengths, interpret=False):
    rows, width = query.shape
    slots = prefix.shape[0]
    full = lambda i, g, s, n: (0, 0)
    grid_spec = pltpu.PrefetchScalarGridSpec(
        num_scalar_prefetch=3,
        grid=(block_groups.shape[0],),
        in_specs=[
            pl.BlockSpec((rows, width), full),
            pl.BlockSpec((rows, width), full),
            pl.BlockSpec((rows, width), full),
            pl.BlockSpec((1, 2, PREFIX, width), lambda i, g, s, n: (g[i], 0, 0, 0)),
        ],
        out_specs=pl.BlockSpec((rows, width), full),
    )
    flops = 4 * 2 * 2 * WINDOW * (PREFIX + WINDOW) * width * block_groups.shape[0]
    return pl.pallas_call(
        attention_kernel,
        grid_spec=grid_spec,
        out_shape=jax.ShapeDtypeStruct((rows, width), jnp.bfloat16),
        compiler_params=pltpu.CompilerParams(dimension_semantics=("arbitrary",)),
        interpret=interpret,
        cost_estimate=pl.CostEstimate(
            flops=flops,
            transcendentals=4 * WINDOW * (PREFIX + WINDOW) * block_groups.shape[0],
            bytes_accessed=slots * 2 * PREFIX * width * 2 + 4 * rows * width * 2,
        ),
    )(
        jnp.clip(block_groups, 0, slots - 1),
        starts,
        block_lengths,
        query,
        keys,
        values,
        prefix,
    )


def slot_ranks(identity, experts):
    flat_ids = identity.reshape(-1)
    hits = (flat_ids[:, None] == jnp.arange(experts, dtype=jnp.int32)[None, :]).astype(jnp.int32)
    before = jnp.cumsum(hits, axis=0) - hits
    return (flat_ids, jnp.sum(before * hits, axis=1))


def slot_table(flat_ids, ranks, capacity, experts, row_count, topk):
    kept = ranks < capacity
    target = jnp.where(kept, flat_ids * capacity + ranks, experts * capacity)
    source = jnp.arange(flat_ids.shape[0], dtype=jnp.int32) // topk
    table = (
        jnp.full((experts * capacity,), row_count, jnp.int32).at[target].set(source, mode="drop")
    )
    return (kept, table)


def expert_apply(slots, weight_in, weight_down):
    joined = jnp.einsum("slcd,ldgh->slcgh", slots, weight_in, preferred_element_type=jnp.float32)
    units = (jax.nn.gelu(joined[:, :, :, 0], approximate=True) * joined[:, :, :, 1]).astype(
        jnp.bfloat16
    )
    return jnp.einsum("slch,lhd->slcd", units, weight_down, preferred_element_type=jnp.float32)


def shards(
    tokens,
    lengths,
    groups,
    owners,
    prefix_cache,
    attn_gain,
    w_qkv,
    w_out,
    moe_gain,
    w_router,
    expert_ids,
    w_in,
    w_down,
):
    rows_whole = lax.all_gather(tokens, "exp", axis=1, tiled=True)
    row_count = rows_whole.shape[0]
    full_width = rows_whole.shape[1]
    quarter = tokens.shape[1]
    local_heads = quarter // HEAD_DIM
    x_attn = norm_rows(rows_whole.astype(jnp.float32), attn_gain).astype(jnp.bfloat16)
    qkv = jnp.dot(
        x_attn, w_qkv.reshape(full_width, 3 * quarter), preferred_element_type=jnp.float32
    )
    qkv = qkv.astype(jnp.bfloat16).reshape(row_count, 3, quarter)
    suffix_kv = jnp.stack([qkv[:, 1], qkv[:, 2]], axis=1)
    own_slot = prefix_cache[0]
    block_lengths = lengths[0]
    block_groups = groups[0]
    starts = jnp.cumsum(block_lengths) - block_lengths
    req_total = lax.axis_size("req")
    pieces = own_slot.reshape(req_total, PREFIX // req_total, 2, quarter)
    pieces = lax.all_to_all(pieces, "req", split_axis=0, concat_axis=0, tiled=True)
    owned = jnp.take(pieces, owners, axis=0)
    cached = lax.all_gather(owned, "req", axis=1, tiled=True)
    cached = jnp.transpose(cached, (0, 2, 1, 3))
    context = attention(
        qkv[:, 0], qkv[:, 1], qkv[:, 2], cached, block_groups, starts, block_lengths
    )
    context_full = lax.all_gather(context, "exp", axis=1, tiled=True)
    exp_total = lax.axis_size("exp")
    w_out_full = lax.all_to_all(
        jnp.broadcast_to(w_out[None], (exp_total,) + w_out.shape),
        "exp",
        split_axis=0,
        concat_axis=0,
        tiled=True,
    ).reshape(exp_total * w_out.shape[0], w_out.shape[1])
    attn_full = jnp.dot(context_full, w_out_full, preferred_element_type=jnp.float32)
    resid_full = rows_whole.astype(jnp.float32) + attn_full
    x_source = norm_rows(resid_full, moe_gain).astype(jnp.bfloat16)
    column_start = lax.axis_index("exp") * quarter
    resid = lax.dynamic_slice_in_dim(resid_full, column_start, quarter, 1)
    logits = jnp.dot(x_source, w_router, preferred_element_type=jnp.float32)
    gates = jax.nn.sigmoid(jnp.take_along_axis(logits, expert_ids, axis=1)).reshape(-1)
    flat_ids, ranks = slot_ranks(expert_ids, EXPERTS)
    kept, table = slot_table(flat_ids, ranks, CAP, EXPERTS, row_count, TOP)
    columns = x_source.shape[1]
    padded = jnp.concatenate([x_source, jnp.zeros((1, columns), x_source.dtype)], axis=0)
    picked = padded[table].reshape(EXPERTS, 1, CAP, columns)
    local_rows = EXPERTS * SPLIT // req_total
    outgoing_rows = jnp.broadcast_to(picked, (EXPERTS, SPLIT, CAP, columns)).reshape(
        req_total, local_rows, CAP, columns
    )
    lanes = 128
    flat_shape = (req_total, local_rows, CAP * columns // lanes, lanes)
    arrived = lax.all_to_all(
        outgoing_rows.reshape(flat_shape), "req", split_axis=0, concat_axis=0, tiled=True
    ).reshape(outgoing_rows.shape)
    partial_out = expert_apply(arrived, w_in, w_down)
    returned = (
        lax.all_to_all(
            partial_out.astype(jnp.bfloat16).reshape(flat_shape),
            "req",
            split_axis=0,
            concat_axis=0,
            tiled=True,
        )
        .reshape(partial_out.shape)
        .astype(partial_out.dtype)
    )
    block_count, _, _, out_columns = returned.shape
    pair_column = flat_ids * (SPLIT * CAP) + jnp.minimum(ranks, CAP - 1)
    pair_scale = jnp.where(kept, gates, 0.0)
    columns_all = lax.broadcasted_iota(jnp.int32, (row_count * TOP, block_count * CAP), 1)
    offset = columns_all - pair_column[:, None]
    hit = (offset == 0) | (offset == CAP)
    selection = jnp.where(hit, pair_scale[:, None], 0.0).reshape(row_count, TOP, -1).sum(axis=1)
    mixture = jnp.dot(
        selection,
        returned.reshape(block_count * CAP, out_columns).astype(jnp.float32),
        precision=lax.Precision.HIGHEST,
        preferred_element_type=jnp.float32,
    )
    blocks = jnp.transpose(
        mixture.astype(jnp.bfloat16).reshape(row_count, exp_total, quarter), (1, 0, 2)
    )
    moe_part = jnp.sum(
        lax.all_to_all(blocks, "exp", split_axis=0, concat_axis=0, tiled=True).astype(
            jnp.float32
        ),
        axis=0,
    )
    hidden_out = (resid + moe_part).astype(jnp.bfloat16)
    return (hidden_out, suffix_kv)


def solution(mesh):
    return jax.shard_map(
        shards,
        mesh=mesh,
        in_specs=(
            P("req", "exp"),
            P("req", None),
            P("req", None),
            P(),
            P("req", None, None, "exp"),
            P(),
            P(None, None, "exp"),
            P("exp", None),
            P(),
            P(),
            P("req", None),
            P("req", None, None, "exp"),
            P("req", "exp", None),
        ),
        out_specs=(P("req", "exp"), P("req", None, "exp")),
        check_vma=False,
    )
```

```python
import math

import jax
import jax.numpy as jnp
from jax import lax
from jax.sharding import PartitionSpec as P
from jax.experimental import pallas as pl
from jax.experimental.pallas import tpu as pltpu

HEAD_DIM = 64
EXPERTS = 16
TOP = 2
SPLIT = 2
GROUPS = 4
PREFIX = 2048
REQ_DEV = 4
SUF_MOST = 128
CAP = 40
WINDOW = SUF_MOST + 16


epsilon = 1e-06


def spread(shard, axis, root):
    mine = lax.axis_index(axis) == root
    return lax.psum(jnp.where(mine, shard, jnp.zeros_like(shard)), axis)


def norm_rows(values, gain):
    squares = jnp.sum(values * values, axis=1)
    return values * lax.rsqrt(squares / values.shape[1] + epsilon)[:, None] * gain


def request_context(query_all, key_all, value_all, prefix_kv, start, length, window):
    row_count = query_all.shape[0]
    first = jnp.minimum(start, row_count - window)
    query_win = lax.dynamic_slice_in_dim(query_all, first, window, 0)
    key_win = lax.dynamic_slice_in_dim(key_all, first, window, 0)
    value_win = lax.dynamic_slice_in_dim(value_all, first, window, 0)
    keys = jnp.concatenate([prefix_kv[:, 0], key_win], axis=0)
    values = jnp.concatenate([prefix_kv[:, 1], value_win], axis=0)
    scores = jnp.einsum(
        "qhd,khd->hqk", query_win, keys, preferred_element_type=jnp.float32
    ) / math.sqrt(query_all.shape[2])
    positions = first + jnp.arange(window, dtype=jnp.int32)
    suffix_ok = (positions[None, :] <= positions[:, None]) & (positions[None, :] >= start)
    allowed = jnp.concatenate([jnp.ones((window, prefix_kv.shape[0]), bool), suffix_ok], axis=1)
    scores = jnp.where(allowed[None], scores, -1e30)
    highest = jnp.max(scores, axis=-1, keepdims=True)
    weight = jnp.exp(scores - highest)
    totals = jnp.sum(weight, axis=-1)
    context = jnp.einsum(
        "hqk,khd->qhd", weight.astype(jnp.bfloat16), values, preferred_element_type=jnp.float32
    )
    context = context / jnp.transpose(totals)[:, :, None]
    inside = (positions >= start) & (positions < start + length)
    context = context * inside[:, None, None].astype(jnp.float32)
    placed = jnp.zeros((row_count,) + context.shape[1:], jnp.float32)
    return lax.dynamic_update_slice_in_dim(placed, context, first, 0)


def attention_kernel(
    group_ref, start_ref, length_ref, query_ref, key_ref, value_ref, prefix_ref, out_ref
):
    request = pl.program_id(0)

    @pl.when(request == 0)
    def _():
        out_ref[...] = jnp.zeros_like(out_ref)

    start = start_ref[request]
    stop = start + length_ref[request]
    total_rows, width = query_ref.shape
    rows = WINDOW
    first = pl.multiple_of(jnp.minimum((start // 16) * 16, total_rows - rows), 16)
    row_ids = first + lax.broadcasted_iota(jnp.int32, (rows, rows), 0)
    col_ids = first + lax.broadcasted_iota(jnp.int32, (rows, rows), 1)
    suffix_ok = (col_ids <= row_ids) & (col_ids >= start)
    lane_head = lax.broadcasted_iota(jnp.int32, (1, width), 1) // HEAD_DIM
    query = query_ref[pl.ds(first, rows), :]
    keys = key_ref[pl.ds(first, rows), :]
    values = value_ref[pl.ds(first, rows), :]
    prefix_keys = prefix_ref[0, 0]
    prefix_values = prefix_ref[0, 1]
    scale = 1.0 / math.sqrt(HEAD_DIM)
    contract = (((1,), (1,)), ((), ()))
    context = jnp.zeros((rows, width), jnp.float32)
    for head in range(width // HEAD_DIM):
        in_head = lane_head == head
        query_h = jnp.where(in_head, query, jnp.zeros_like(query))
        score_pre = lax.dot_general(
            query_h, prefix_keys, contract, preferred_element_type=jnp.float32
        ) * scale
        score_suf = lax.dot_general(
            query_h, keys, contract, preferred_element_type=jnp.float32
        ) * scale
        score_suf = jnp.where(suffix_ok, score_suf, -1e30)
        highest = jnp.maximum(
            jnp.max(score_pre, axis=1, keepdims=True), jnp.max(score_suf, axis=1, keepdims=True)
        )
        weight_pre = jnp.exp(score_pre - highest)
        weight_suf = jnp.exp(score_suf - highest)
        totals = jnp.sum(weight_pre, axis=1, keepdims=True) + jnp.sum(
            weight_suf, axis=1, keepdims=True
        )
        mixed = jnp.dot(
            weight_pre.astype(jnp.bfloat16), prefix_values, preferred_element_type=jnp.float32
        ) + jnp.dot(weight_suf.astype(jnp.bfloat16), values, preferred_element_type=jnp.float32)
        context = context + jnp.where(in_head, mixed / totals, 0.0)
    row_in = first + lax.broadcasted_iota(jnp.int32, (rows, 1), 0)
    inside = (row_in >= start) & (row_in < stop)
    out_ref[pl.ds(first, rows), :] = jnp.where(
        inside, context.astype(out_ref.dtype), out_ref[pl.ds(first, rows), :]
    )


def attention(query, keys, values, prefix, block_groups, starts, block_lengths, interpret=False):
    rows, width = query.shape
    slots = prefix.shape[0]
    full = lambda i, g, s, n: (0, 0)
    grid_spec = pltpu.PrefetchScalarGridSpec(
        num_scalar_prefetch=3,
        grid=(block_groups.shape[0],),
        in_specs=[
            pl.BlockSpec((rows, width), full),
            pl.BlockSpec((rows, width), full),
            pl.BlockSpec((rows, width), full),
            pl.BlockSpec((1, 2, PREFIX, width), lambda i, g, s, n: (g[i], 0, 0, 0)),
        ],
        out_specs=pl.BlockSpec((rows, width), full),
    )
    flops = 4 * 2 * 2 * WINDOW * (PREFIX + WINDOW) * width * block_groups.shape[0]
    return pl.pallas_call(
        attention_kernel,
        grid_spec=grid_spec,
        out_shape=jax.ShapeDtypeStruct((rows, width), jnp.bfloat16),
        compiler_params=pltpu.CompilerParams(dimension_semantics=("arbitrary",)),
        interpret=interpret,
        cost_estimate=pl.CostEstimate(
            flops=flops,
            transcendentals=4 * WINDOW * (PREFIX + WINDOW) * block_groups.shape[0],
            bytes_accessed=slots * 2 * PREFIX * width * 2 + 4 * rows * width * 2,
        ),
    )(
        jnp.clip(block_groups, 0, slots - 1),
        starts,
        block_lengths,
        query,
        keys,
        values,
        prefix,
    )


def slot_ranks(identity, experts):
    flat_ids = identity.reshape(-1)
    hits = (flat_ids[:, None] == jnp.arange(experts, dtype=jnp.int32)[None, :]).astype(jnp.int32)
    before = jnp.cumsum(hits, axis=0) - hits
    return (flat_ids, jnp.sum(before * hits, axis=1))


def slot_table(flat_ids, ranks, capacity, experts, row_count, topk):
    kept = ranks < capacity
    target = jnp.where(kept, flat_ids * capacity + ranks, experts * capacity)
    source = jnp.arange(flat_ids.shape[0], dtype=jnp.int32) // topk
    table = (
        jnp.full((experts * capacity,), row_count, jnp.int32).at[target].set(source, mode="drop")
    )
    return (kept, table)


def expert_apply(slots, weight_in, weight_down):
    joined = jnp.einsum("slcd,ldgh->slcgh", slots, weight_in, preferred_element_type=jnp.float32)
    units = (jax.nn.gelu(joined[:, :, :, 0], approximate=True) * joined[:, :, :, 1]).astype(
        jnp.bfloat16
    )
    return jnp.einsum("slch,lhd->slcd", units, weight_down, preferred_element_type=jnp.float32)


def shards(
    tokens,
    lengths,
    groups,
    owners,
    prefix_cache,
    attn_gain,
    w_qkv,
    w_out,
    moe_gain,
    w_router,
    expert_ids,
    w_in,
    w_down,
):
    rows_whole = lax.all_gather(tokens, "exp", axis=1, tiled=True)
    row_count = rows_whole.shape[0]
    full_width = rows_whole.shape[1]
    quarter = tokens.shape[1]
    local_heads = quarter // HEAD_DIM
    x_attn = norm_rows(rows_whole.astype(jnp.float32), attn_gain).astype(jnp.bfloat16)
    qkv = jnp.dot(
        x_attn, w_qkv.reshape(full_width, 3 * quarter), preferred_element_type=jnp.float32
    )
    qkv = qkv.astype(jnp.bfloat16).reshape(row_count, 3, quarter)
    suffix_kv = jnp.stack([qkv[:, 1], qkv[:, 2]], axis=1)
    own_slot = prefix_cache[0]
    block_lengths = lengths[0]
    block_groups = groups[0]
    starts = jnp.cumsum(block_lengths) - block_lengths
    req_total = lax.axis_size("req")
    pieces = own_slot.reshape(req_total, PREFIX // req_total, 2, quarter)
    pieces = lax.all_to_all(pieces, "req", split_axis=0, concat_axis=0, tiled=True)
    owned = jnp.take(pieces, owners, axis=0)
    cached = lax.all_gather(owned, "req", axis=1, tiled=True)
    cached = jnp.transpose(cached, (0, 2, 1, 3))
    context = attention(
        qkv[:, 0], qkv[:, 1], qkv[:, 2], cached, block_groups, starts, block_lengths
    )
    context_full = lax.all_gather(context, "exp", axis=1, tiled=True)
    exp_total = lax.axis_size("exp")
    w_out_full = lax.all_to_all(
        jnp.broadcast_to(w_out[None], (exp_total,) + w_out.shape),
        "exp",
        split_axis=0,
        concat_axis=0,
        tiled=True,
    ).reshape(exp_total * w_out.shape[0], w_out.shape[1])
    attn_full = jnp.dot(context_full, w_out_full, preferred_element_type=jnp.float32)
    resid_full = rows_whole.astype(jnp.float32) + attn_full
    x_source = norm_rows(resid_full, moe_gain).astype(jnp.bfloat16)
    column_start = lax.axis_index("exp") * quarter
    resid = lax.dynamic_slice_in_dim(resid_full, column_start, quarter, 1)
    logits = jnp.dot(x_source, w_router, preferred_element_type=jnp.float32)
    gates = jax.nn.sigmoid(jnp.take_along_axis(logits, expert_ids, axis=1)).reshape(-1)
    flat_ids, ranks = slot_ranks(expert_ids, EXPERTS)
    kept, table = slot_table(flat_ids, ranks, CAP, EXPERTS, row_count, TOP)
    columns = x_source.shape[1]
    padded = jnp.concatenate([x_source, jnp.zeros((1, columns), x_source.dtype)], axis=0)
    picked = padded[table].reshape(EXPERTS, 1, CAP, columns)
    local_rows = EXPERTS * SPLIT // req_total
    outgoing_rows = jnp.broadcast_to(picked, (EXPERTS, SPLIT, CAP, columns)).reshape(
        req_total, local_rows, CAP, columns
    )
    own_index = lax.axis_index("req")
    shifts = jnp.arange(req_total, dtype=jnp.int32)
    rolled = jnp.take(outgoing_rows, (own_index + shifts) % req_total, axis=0)
    arrived = [rolled[0]]
    for shift in range(1, req_total):
        arrived.append(
            lax.ppermute(
                rolled[shift], "req", [(i, (i + shift) % req_total) for i in range(req_total)]
            )
        )
    partial_out = expert_apply(jnp.stack(arrived, axis=0), w_in, w_down)
    partial_out = jnp.take(partial_out, (own_index - shifts) % req_total, axis=0)
    returned = lax.all_to_all(
        partial_out.astype(jnp.bfloat16), "req", split_axis=0, concat_axis=0, tiled=True
    ).astype(partial_out.dtype)
    block_count, _, _, out_columns = returned.shape
    pair_column = flat_ids * (SPLIT * CAP) + jnp.minimum(ranks, CAP - 1)
    pair_scale = jnp.where(kept, gates, 0.0)
    columns_all = lax.broadcasted_iota(jnp.int32, (row_count * TOP, block_count * CAP), 1)
    offset = columns_all - pair_column[:, None]
    hit = (offset == 0) | (offset == CAP)
    selection = jnp.where(hit, pair_scale[:, None], 0.0).reshape(row_count, TOP, -1).sum(axis=1)
    mixture = jnp.dot(
        selection,
        returned.reshape(block_count * CAP, out_columns).astype(jnp.float32),
        precision=lax.Precision.HIGHEST,
        preferred_element_type=jnp.float32,
    )
    blocks = jnp.transpose(
        mixture.astype(jnp.bfloat16).reshape(row_count, exp_total, quarter), (1, 0, 2)
    )
    moe_part = jnp.sum(
        lax.all_to_all(blocks, "exp", split_axis=0, concat_axis=0, tiled=True).astype(
            jnp.float32
        ),
        axis=0,
    )
    hidden_out = (resid + moe_part).astype(jnp.bfloat16)
    return (hidden_out, suffix_kv)


def solution(mesh):
    return jax.shard_map(
        shards,
        mesh=mesh,
        in_specs=(
            P("req", "exp"),
            P("req", None),
            P("req", None),
            P(),
            P("req", None, None, "exp"),
            P(),
            P(None, None, "exp"),
            P("exp", None),
            P(),
            P(),
            P("req", None),
            P("req", None, None, "exp"),
            P("req", "exp", None),
        ),
        out_specs=(P("req", "exp"), P("req", None, "exp")),
        check_vma=False,
    )
```

```python
import math

import jax
import jax.numpy as jnp
from jax import lax
from jax.sharding import PartitionSpec as P
from jax.experimental import pallas as pl
from jax.experimental.pallas import tpu as pltpu

HEAD_DIM = 64
EXPERTS = 16
TOP = 2
SPLIT = 2
GROUPS = 4
PREFIX = 2048
REQ_DEV = 4
SUF_MOST = 128
CAP = 40
WINDOW = SUF_MOST + 16


epsilon = 1e-06


def spread(shard, axis, root):
    mine = lax.axis_index(axis) == root
    return lax.psum(jnp.where(mine, shard, jnp.zeros_like(shard)), axis)


def norm_rows(values, gain):
    squares = jnp.sum(values * values, axis=1)
    return values * lax.rsqrt(squares / values.shape[1] + epsilon)[:, None] * gain


def request_context(query_all, key_all, value_all, prefix_kv, start, length, window):
    row_count = query_all.shape[0]
    first = jnp.minimum(start, row_count - window)
    query_win = lax.dynamic_slice_in_dim(query_all, first, window, 0)
    key_win = lax.dynamic_slice_in_dim(key_all, first, window, 0)
    value_win = lax.dynamic_slice_in_dim(value_all, first, window, 0)
    keys = jnp.concatenate([prefix_kv[:, 0], key_win], axis=0)
    values = jnp.concatenate([prefix_kv[:, 1], value_win], axis=0)
    scores = jnp.einsum(
        "qhd,khd->hqk", query_win, keys, preferred_element_type=jnp.float32
    ) / math.sqrt(query_all.shape[2])
    positions = first + jnp.arange(window, dtype=jnp.int32)
    suffix_ok = (positions[None, :] <= positions[:, None]) & (positions[None, :] >= start)
    allowed = jnp.concatenate([jnp.ones((window, prefix_kv.shape[0]), bool), suffix_ok], axis=1)
    scores = jnp.where(allowed[None], scores, -1e30)
    highest = jnp.max(scores, axis=-1, keepdims=True)
    weight = jnp.exp(scores - highest)
    totals = jnp.sum(weight, axis=-1)
    context = jnp.einsum(
        "hqk,khd->qhd", weight.astype(jnp.bfloat16), values, preferred_element_type=jnp.float32
    )
    context = context / jnp.transpose(totals)[:, :, None]
    inside = (positions >= start) & (positions < start + length)
    context = context * inside[:, None, None].astype(jnp.float32)
    placed = jnp.zeros((row_count,) + context.shape[1:], jnp.float32)
    return lax.dynamic_update_slice_in_dim(placed, context, first, 0)


def attention_kernel(
    group_ref, start_ref, length_ref, query_ref, key_ref, value_ref, prefix_ref, out_ref
):
    request = pl.program_id(0)

    @pl.when(request == 0)
    def _():
        out_ref[...] = jnp.zeros_like(out_ref)

    start = start_ref[request]
    stop = start + length_ref[request]
    total_rows, width = query_ref.shape
    rows = WINDOW
    first = pl.multiple_of(jnp.minimum((start // 16) * 16, total_rows - rows), 16)
    row_ids = first + lax.broadcasted_iota(jnp.int32, (rows, rows), 0)
    col_ids = first + lax.broadcasted_iota(jnp.int32, (rows, rows), 1)
    suffix_ok = (col_ids <= row_ids) & (col_ids >= start)
    lane_head = lax.broadcasted_iota(jnp.int32, (1, width), 1) // HEAD_DIM
    query = query_ref[pl.ds(first, rows), :]
    keys = key_ref[pl.ds(first, rows), :]
    values = value_ref[pl.ds(first, rows), :]
    prefix_keys = prefix_ref[0, 0]
    prefix_values = prefix_ref[0, 1]
    scale = 1.0 / math.sqrt(HEAD_DIM)
    contract = (((1,), (1,)), ((), ()))
    context = jnp.zeros((rows, width), jnp.float32)
    for head in range(width // HEAD_DIM):
        in_head = lane_head == head
        query_h = jnp.where(in_head, query, jnp.zeros_like(query))
        score_pre = lax.dot_general(
            query_h, prefix_keys, contract, preferred_element_type=jnp.float32
        ) * scale
        score_suf = lax.dot_general(
            query_h, keys, contract, preferred_element_type=jnp.float32
        ) * scale
        score_suf = jnp.where(suffix_ok, score_suf, -1e30)
        highest = jnp.maximum(
            jnp.max(score_pre, axis=1, keepdims=True), jnp.max(score_suf, axis=1, keepdims=True)
        )
        weight_pre = jnp.exp(score_pre - highest)
        weight_suf = jnp.exp(score_suf - highest)
        totals = jnp.sum(weight_pre, axis=1, keepdims=True) + jnp.sum(
            weight_suf, axis=1, keepdims=True
        )
        mixed = jnp.dot(
            weight_pre.astype(jnp.bfloat16), prefix_values, preferred_element_type=jnp.float32
        ) + jnp.dot(weight_suf.astype(jnp.bfloat16), values, preferred_element_type=jnp.float32)
        context = context + jnp.where(in_head, mixed / totals, 0.0)
    row_in = first + lax.broadcasted_iota(jnp.int32, (rows, 1), 0)
    inside = (row_in >= start) & (row_in < stop)
    out_ref[pl.ds(first, rows), :] = jnp.where(
        inside, context.astype(out_ref.dtype), out_ref[pl.ds(first, rows), :]
    )


def attention(query, keys, values, prefix, block_groups, starts, block_lengths, interpret=False):
    rows, width = query.shape
    slots = prefix.shape[0]
    full = lambda i, g, s, n: (0, 0)
    grid_spec = pltpu.PrefetchScalarGridSpec(
        num_scalar_prefetch=3,
        grid=(block_groups.shape[0],),
        in_specs=[
            pl.BlockSpec((rows, width), full),
            pl.BlockSpec((rows, width), full),
            pl.BlockSpec((rows, width), full),
            pl.BlockSpec((1, 2, PREFIX, width), lambda i, g, s, n: (g[i], 0, 0, 0)),
        ],
        out_specs=pl.BlockSpec((rows, width), full),
    )
    flops = 4 * 2 * 2 * WINDOW * (PREFIX + WINDOW) * width * block_groups.shape[0]
    return pl.pallas_call(
        attention_kernel,
        grid_spec=grid_spec,
        out_shape=jax.ShapeDtypeStruct((rows, width), jnp.bfloat16),
        compiler_params=pltpu.CompilerParams(dimension_semantics=("arbitrary",)),
        interpret=interpret,
        cost_estimate=pl.CostEstimate(
            flops=flops,
            transcendentals=4 * WINDOW * (PREFIX + WINDOW) * block_groups.shape[0],
            bytes_accessed=slots * 2 * PREFIX * width * 2 + 4 * rows * width * 2,
        ),
    )(
        jnp.clip(block_groups, 0, slots - 1),
        starts,
        block_lengths,
        query,
        keys,
        values,
        prefix,
    )


def slot_ranks(identity, experts):
    flat_ids = identity.reshape(-1)
    hits = (flat_ids[:, None] == jnp.arange(experts, dtype=jnp.int32)[None, :]).astype(jnp.int32)
    before = jnp.cumsum(hits, axis=0) - hits
    return (flat_ids, jnp.sum(before * hits, axis=1))


def slot_table(flat_ids, ranks, capacity, experts, row_count, topk):
    kept = ranks < capacity
    target = jnp.where(kept, flat_ids * capacity + ranks, experts * capacity)
    source = jnp.arange(flat_ids.shape[0], dtype=jnp.int32) // topk
    table = (
        jnp.full((experts * capacity,), row_count, jnp.int32).at[target].set(source, mode="drop")
    )
    return (kept, table)


def expert_apply(slots, weight_in, weight_down):
    joined = jnp.einsum("slcd,ldgh->slcgh", slots, weight_in, preferred_element_type=jnp.float32)
    units = (jax.nn.gelu(joined[:, :, :, 0], approximate=True) * joined[:, :, :, 1]).astype(
        jnp.bfloat16
    )
    return jnp.einsum("slch,lhd->slcd", units, weight_down, preferred_element_type=jnp.float32)


def shards(
    tokens,
    lengths,
    groups,
    owners,
    prefix_cache,
    attn_gain,
    w_qkv,
    w_out,
    moe_gain,
    w_router,
    expert_ids,
    w_in,
    w_down,
):
    rows_whole = lax.all_gather(tokens, "exp", axis=1, tiled=True)
    row_count = rows_whole.shape[0]
    full_width = rows_whole.shape[1]
    quarter = tokens.shape[1]
    local_heads = quarter // HEAD_DIM
    x_attn = norm_rows(rows_whole.astype(jnp.float32), attn_gain).astype(jnp.bfloat16)
    qkv = jnp.dot(
        x_attn, w_qkv.reshape(full_width, 3 * quarter), preferred_element_type=jnp.float32
    )
    qkv = qkv.astype(jnp.bfloat16).reshape(row_count, 3, quarter)
    suffix_kv = jnp.stack([qkv[:, 1], qkv[:, 2]], axis=1)
    own_slot = prefix_cache[0]
    block_lengths = lengths[0]
    block_groups = groups[0]
    starts = jnp.cumsum(block_lengths) - block_lengths
    req_total = lax.axis_size("req")
    pieces = own_slot.reshape(req_total, PREFIX // req_total, 2, quarter)
    pieces = lax.all_to_all(pieces, "req", split_axis=0, concat_axis=0, tiled=True)
    owned = jnp.take(pieces, owners, axis=0)
    cached = lax.all_gather(owned, "req", axis=1, tiled=True)
    cached = jnp.transpose(cached, (0, 2, 1, 3))
    context = attention(
        qkv[:, 0], qkv[:, 1], qkv[:, 2], cached, block_groups, starts, block_lengths
    )
    context_full = lax.all_gather(context, "exp", axis=1, tiled=True)
    exp_total = lax.axis_size("exp")
    w_out_full = lax.all_to_all(
        jnp.broadcast_to(w_out[None], (exp_total,) + w_out.shape),
        "exp",
        split_axis=0,
        concat_axis=0,
        tiled=True,
    ).reshape(exp_total * w_out.shape[0], w_out.shape[1])
    attn_full = jnp.dot(context_full, w_out_full, preferred_element_type=jnp.float32)
    resid_full = rows_whole.astype(jnp.float32) + attn_full
    x_source = norm_rows(resid_full, moe_gain).astype(jnp.bfloat16)
    column_start = lax.axis_index("exp") * quarter
    resid = lax.dynamic_slice_in_dim(resid_full, column_start, quarter, 1)
    logits = jnp.dot(x_source, w_router, preferred_element_type=jnp.float32)
    gates = jax.nn.sigmoid(jnp.take_along_axis(logits, expert_ids, axis=1)).reshape(-1)
    flat_ids, ranks = slot_ranks(expert_ids, EXPERTS)
    kept, table = slot_table(flat_ids, ranks, CAP, EXPERTS, row_count, TOP)
    columns = x_source.shape[1]
    padded = jnp.concatenate([x_source, jnp.zeros((1, columns), x_source.dtype)], axis=0)
    picked = padded[table].reshape(EXPERTS, 1, CAP, columns)
    local_rows = EXPERTS * SPLIT // req_total
    outgoing_rows = jnp.broadcast_to(picked, (EXPERTS, SPLIT, CAP, columns)).reshape(
        req_total, local_rows, CAP, columns
    )
    partial_out = expert_apply(
        lax.all_to_all(outgoing_rows, "req", split_axis=0, concat_axis=0, tiled=True), w_in, w_down
    )
    returned = lax.all_to_all(
        partial_out.astype(jnp.bfloat16), "req", split_axis=0, concat_axis=0, tiled=True
    ).astype(partial_out.dtype)
    block_count, _, _, out_columns = returned.shape
    pair_column = flat_ids * (SPLIT * CAP) + jnp.minimum(ranks, CAP - 1)
    pair_scale = jnp.where(kept, gates, 0.0)
    columns_all = lax.broadcasted_iota(jnp.int32, (row_count * TOP, block_count * CAP), 1)
    offset = columns_all - pair_column[:, None]
    hit = (offset == 0) | (offset == CAP)
    selection = jnp.where(hit, pair_scale[:, None], 0.0).reshape(row_count, TOP, -1).sum(axis=1)
    mixture = jnp.dot(
        selection,
        returned.reshape(block_count * CAP, out_columns).astype(jnp.float32),
        precision=lax.Precision.HIGH,
        preferred_element_type=jnp.float32,
    )
    blocks = jnp.transpose(
        mixture.astype(jnp.bfloat16).reshape(row_count, exp_total, quarter), (1, 0, 2)
    )
    moe_part = jnp.sum(
        lax.all_to_all(blocks, "exp", split_axis=0, concat_axis=0, tiled=True).astype(
            jnp.float32
        ),
        axis=0,
    )
    hidden_out = (resid + moe_part).astype(jnp.bfloat16)
    return (hidden_out, suffix_kv)


def solution(mesh):
    return jax.shard_map(
        shards,
        mesh=mesh,
        in_specs=(
            P("req", "exp"),
            P("req", None),
            P("req", None),
            P(),
            P("req", None, None, "exp"),
            P(),
            P(None, None, "exp"),
            P("exp", None),
            P(),
            P(),
            P("req", None),
            P("req", None, None, "exp"),
            P("req", "exp", None),
        ),
        out_specs=(P("req", "exp"), P("req", None, "exp")),
        check_vma=False,
    )
```

```python
import math

import jax
import jax.numpy as jnp
from jax import lax
from jax.sharding import PartitionSpec as P
from jax.experimental import pallas as pl
from jax.experimental.pallas import tpu as pltpu

HEAD_DIM = 64
EXPERTS = 16
TOP = 2
SPLIT = 2
GROUPS = 4
PREFIX = 2048
REQ_DEV = 4
SUF_MOST = 128
CAP = 40
WINDOW = SUF_MOST + 16


epsilon = 1e-06


def spread(shard, axis, root):
    mine = lax.axis_index(axis) == root
    return lax.psum(jnp.where(mine, shard, jnp.zeros_like(shard)), axis)


def norm_rows(values, gain):
    squares = jnp.sum(values * values, axis=1)
    return values * lax.rsqrt(squares / values.shape[1] + epsilon)[:, None] * gain


def request_context(query_all, key_all, value_all, prefix_kv, start, length, window):
    row_count = query_all.shape[0]
    first = jnp.minimum(start, row_count - window)
    query_win = lax.dynamic_slice_in_dim(query_all, first, window, 0)
    key_win = lax.dynamic_slice_in_dim(key_all, first, window, 0)
    value_win = lax.dynamic_slice_in_dim(value_all, first, window, 0)
    keys = jnp.concatenate([prefix_kv[:, 0], key_win], axis=0)
    values = jnp.concatenate([prefix_kv[:, 1], value_win], axis=0)
    scores = jnp.einsum(
        "qhd,khd->hqk", query_win, keys, preferred_element_type=jnp.float32
    ) / math.sqrt(query_all.shape[2])
    positions = first + jnp.arange(window, dtype=jnp.int32)
    suffix_ok = (positions[None, :] <= positions[:, None]) & (positions[None, :] >= start)
    allowed = jnp.concatenate([jnp.ones((window, prefix_kv.shape[0]), bool), suffix_ok], axis=1)
    scores = jnp.where(allowed[None], scores, -1e30)
    highest = jnp.max(scores, axis=-1, keepdims=True)
    weight = jnp.exp(scores - highest)
    totals = jnp.sum(weight, axis=-1)
    context = jnp.einsum(
        "hqk,khd->qhd", weight.astype(jnp.bfloat16), values, preferred_element_type=jnp.float32
    )
    context = context / jnp.transpose(totals)[:, :, None]
    inside = (positions >= start) & (positions < start + length)
    context = context * inside[:, None, None].astype(jnp.float32)
    placed = jnp.zeros((row_count,) + context.shape[1:], jnp.float32)
    return lax.dynamic_update_slice_in_dim(placed, context, first, 0)


def attention_kernel(
    group_ref, start_ref, length_ref, query_ref, key_ref, value_ref, prefix_ref, out_ref
):
    request = pl.program_id(0)

    @pl.when(request == 0)
    def _():
        out_ref[...] = jnp.zeros_like(out_ref)

    start = start_ref[request]
    stop = start + length_ref[request]
    total_rows, width = query_ref.shape
    rows = WINDOW
    first = pl.multiple_of(jnp.minimum((start // 16) * 16, total_rows - rows), 16)
    row_ids = first + lax.broadcasted_iota(jnp.int32, (rows, rows), 0)
    col_ids = first + lax.broadcasted_iota(jnp.int32, (rows, rows), 1)
    suffix_ok = (col_ids <= row_ids) & (col_ids >= start)
    lane_head = lax.broadcasted_iota(jnp.int32, (1, width), 1) // HEAD_DIM
    query = query_ref[pl.ds(first, rows), :]
    keys = key_ref[pl.ds(first, rows), :]
    values = value_ref[pl.ds(first, rows), :]
    prefix_keys = prefix_ref[0, 0]
    prefix_values = prefix_ref[0, 1]
    scale = 1.0 / math.sqrt(HEAD_DIM)
    contract = (((1,), (1,)), ((), ()))
    context = jnp.zeros((rows, width), jnp.float32)
    for head in range(width // HEAD_DIM):
        in_head = lane_head == head
        query_h = jnp.where(in_head, query * jnp.asarray(scale, query.dtype), jnp.zeros_like(query))
        score_pre = lax.dot_general(
            query_h, prefix_keys, contract, preferred_element_type=jnp.float32
        )
        score_suf = lax.dot_general(query_h, keys, contract, preferred_element_type=jnp.float32)
        score_suf = jnp.where(suffix_ok, score_suf, -1e30)
        highest = jnp.maximum(
            jnp.max(score_pre, axis=1, keepdims=True), jnp.max(score_suf, axis=1, keepdims=True)
        )
        weight_pre = jnp.exp(score_pre - highest)
        weight_suf = jnp.exp(score_suf - highest)
        totals = jnp.sum(weight_pre, axis=1, keepdims=True) + jnp.sum(
            weight_suf, axis=1, keepdims=True
        )
        mixed = jnp.dot(
            weight_pre.astype(jnp.bfloat16), prefix_values, preferred_element_type=jnp.float32
        ) + jnp.dot(weight_suf.astype(jnp.bfloat16), values, preferred_element_type=jnp.float32)
        context = context + jnp.where(in_head, mixed / totals, 0.0)
    row_in = first + lax.broadcasted_iota(jnp.int32, (rows, 1), 0)
    inside = (row_in >= start) & (row_in < stop)
    out_ref[pl.ds(first, rows), :] = jnp.where(
        inside, context.astype(out_ref.dtype), out_ref[pl.ds(first, rows), :]
    )


def attention(query, keys, values, prefix, block_groups, starts, block_lengths, interpret=False):
    rows, width = query.shape
    slots = prefix.shape[0]
    full = lambda i, g, s, n: (0, 0)
    grid_spec = pltpu.PrefetchScalarGridSpec(
        num_scalar_prefetch=3,
        grid=(block_groups.shape[0],),
        in_specs=[
            pl.BlockSpec((rows, width), full),
            pl.BlockSpec((rows, width), full),
            pl.BlockSpec((rows, width), full),
            pl.BlockSpec((1, 2, PREFIX, width), lambda i, g, s, n: (g[i], 0, 0, 0)),
        ],
        out_specs=pl.BlockSpec((rows, width), full),
    )
    flops = 4 * 2 * 2 * WINDOW * (PREFIX + WINDOW) * width * block_groups.shape[0]
    return pl.pallas_call(
        attention_kernel,
        grid_spec=grid_spec,
        out_shape=jax.ShapeDtypeStruct((rows, width), jnp.bfloat16),
        compiler_params=pltpu.CompilerParams(dimension_semantics=("arbitrary",)),
        interpret=interpret,
        cost_estimate=pl.CostEstimate(
            flops=flops,
            transcendentals=4 * WINDOW * (PREFIX + WINDOW) * block_groups.shape[0],
            bytes_accessed=slots * 2 * PREFIX * width * 2 + 4 * rows * width * 2,
        ),
    )(
        jnp.clip(block_groups, 0, slots - 1),
        starts,
        block_lengths,
        query,
        keys,
        values,
        prefix,
    )


def slot_ranks(identity, experts):
    flat_ids = identity.reshape(-1)
    hits = (flat_ids[:, None] == jnp.arange(experts, dtype=jnp.int32)[None, :]).astype(jnp.int32)
    before = jnp.cumsum(hits, axis=0) - hits
    return (flat_ids, jnp.sum(before * hits, axis=1))


def slot_table(flat_ids, ranks, capacity, experts, row_count, topk):
    kept = ranks < capacity
    target = jnp.where(kept, flat_ids * capacity + ranks, experts * capacity)
    source = jnp.arange(flat_ids.shape[0], dtype=jnp.int32) // topk
    table = (
        jnp.full((experts * capacity,), row_count, jnp.int32).at[target].set(source, mode="drop")
    )
    return (kept, table)


def expert_apply(slots, weight_in, weight_down):
    joined = jnp.einsum("slcd,ldgh->slcgh", slots, weight_in, preferred_element_type=jnp.float32)
    units = (jax.nn.gelu(joined[:, :, :, 0], approximate=True) * joined[:, :, :, 1]).astype(
        jnp.bfloat16
    )
    return jnp.einsum("slch,lhd->slcd", units, weight_down, preferred_element_type=jnp.float32)


def shards(
    tokens,
    lengths,
    groups,
    owners,
    prefix_cache,
    attn_gain,
    w_qkv,
    w_out,
    moe_gain,
    w_router,
    expert_ids,
    w_in,
    w_down,
):
    rows_whole = lax.all_gather(tokens, "exp", axis=1, tiled=True)
    row_count = rows_whole.shape[0]
    full_width = rows_whole.shape[1]
    quarter = tokens.shape[1]
    local_heads = quarter // HEAD_DIM
    x_attn = norm_rows(rows_whole.astype(jnp.float32), attn_gain).astype(jnp.bfloat16)
    qkv = jnp.dot(
        x_attn, w_qkv.reshape(full_width, 3 * quarter), preferred_element_type=jnp.float32
    )
    qkv = qkv.astype(jnp.bfloat16).reshape(row_count, 3, quarter)
    suffix_kv = jnp.stack([qkv[:, 1], qkv[:, 2]], axis=1)
    own_slot = prefix_cache[0]
    block_lengths = lengths[0]
    block_groups = groups[0]
    starts = jnp.cumsum(block_lengths) - block_lengths
    req_total = lax.axis_size("req")
    pieces = own_slot.reshape(req_total, PREFIX // req_total, 2, quarter)
    pieces = lax.all_to_all(pieces, "req", split_axis=0, concat_axis=0, tiled=True)
    owned = jnp.take(pieces, owners, axis=0)
    cached = lax.all_gather(owned, "req", axis=1, tiled=True)
    cached = jnp.transpose(cached, (0, 2, 1, 3))
    context = attention(
        qkv[:, 0], qkv[:, 1], qkv[:, 2], cached, block_groups, starts, block_lengths
    )
    context_full = lax.all_gather(context, "exp", axis=1, tiled=True)
    exp_total = lax.axis_size("exp")
    w_out_full = lax.all_to_all(
        jnp.broadcast_to(w_out[None], (exp_total,) + w_out.shape),
        "exp",
        split_axis=0,
        concat_axis=0,
        tiled=True,
    ).reshape(exp_total * w_out.shape[0], w_out.shape[1])
    attn_full = jnp.dot(context_full, w_out_full, preferred_element_type=jnp.float32)
    resid_full = rows_whole.astype(jnp.float32) + attn_full
    x_source = norm_rows(resid_full, moe_gain).astype(jnp.bfloat16)
    column_start = lax.axis_index("exp") * quarter
    resid = lax.dynamic_slice_in_dim(resid_full, column_start, quarter, 1)
    logits = jnp.dot(x_source, w_router, preferred_element_type=jnp.float32)
    gates = jax.nn.sigmoid(jnp.take_along_axis(logits, expert_ids, axis=1)).reshape(-1)
    flat_ids, ranks = slot_ranks(expert_ids, EXPERTS)
    kept, table = slot_table(flat_ids, ranks, CAP, EXPERTS, row_count, TOP)
    columns = x_source.shape[1]
    padded = jnp.concatenate([x_source, jnp.zeros((1, columns), x_source.dtype)], axis=0)
    picked = padded[table].reshape(EXPERTS, 1, CAP, columns)
    local_rows = EXPERTS * SPLIT // req_total
    outgoing_rows = jnp.broadcast_to(picked, (EXPERTS, SPLIT, CAP, columns)).reshape(
        req_total, local_rows, CAP, columns
    )
    partial_out = expert_apply(
        lax.all_to_all(outgoing_rows, "req", split_axis=0, concat_axis=0, tiled=True), w_in, w_down
    )
    returned = lax.all_to_all(
        partial_out.astype(jnp.bfloat16), "req", split_axis=0, concat_axis=0, tiled=True
    ).astype(partial_out.dtype)
    block_count, _, _, out_columns = returned.shape
    pair_column = flat_ids * (SPLIT * CAP) + jnp.minimum(ranks, CAP - 1)
    pair_scale = jnp.where(kept, gates, 0.0)
    columns_all = lax.broadcasted_iota(jnp.int32, (row_count * TOP, block_count * CAP), 1)
    offset = columns_all - pair_column[:, None]
    hit = (offset == 0) | (offset == CAP)
    selection = jnp.where(hit, pair_scale[:, None], 0.0).reshape(row_count, TOP, -1).sum(axis=1)
    mixture = jnp.dot(
        selection,
        returned.reshape(block_count * CAP, out_columns).astype(jnp.float32),
        precision=lax.Precision.HIGH,
        preferred_element_type=jnp.float32,
    )
    blocks = jnp.transpose(
        mixture.astype(jnp.bfloat16).reshape(row_count, exp_total, quarter), (1, 0, 2)
    )
    moe_part = jnp.sum(
        lax.all_to_all(blocks, "exp", split_axis=0, concat_axis=0, tiled=True).astype(
            jnp.float32
        ),
        axis=0,
    )
    hidden_out = (resid + moe_part).astype(jnp.bfloat16)
    return (hidden_out, suffix_kv)


def solution(mesh):
    return jax.shard_map(
        shards,
        mesh=mesh,
        in_specs=(
            P("req", "exp"),
            P("req", None),
            P("req", None),
            P(),
            P("req", None, None, "exp"),
            P(),
            P(None, None, "exp"),
            P("exp", None),
            P(),
            P(),
            P("req", None),
            P("req", None, None, "exp"),
            P("req", "exp", None),
        ),
        out_specs=(P("req", "exp"), P("req", None, "exp")),
        check_vma=False,
    )
```
